32 devices in a mesh: row: 8 (over y, x, core), col: 4 (over z).
Axes of the slice: x: 2, y: 2, z: 4, core: 2. Of those that a mesh axis runs over, the one named last changes fastest.
Arguments:
- a_matrix: float32 [2, 8, 128, 4, 4, 128], P(None, 'row', None, None, 'col'), may hold values from -24 to 24, as said below
- l_panels: float32 [2, 8, 128, 256], P(None, 'row'), may hold values from -0.25 to 0.25
- linv: float32 [2, 128, 128], replicated, may hold values from -0.13258252 to 1.6, as said below
Outputs:
- c_matrix: float32 [2, 8, 128, 4, 4, 128], P(None, 'row', None, None, 'col')
The draws below stay inside these ranges and needn't reach their ends.
Inputs may be any that keep to these rules, and one draw needn't show every extreme that they name: a_matrix is symmetric as an 2048 x 2048 matrix. Each linv[p] is lower triangular with diagonal entries from 0.8 to 1.6.
All inputs are finite; a program needn't handle non-finite values.
Results may differ from the reference program's by a relative error of at most 0.0001.
Values sent between devices are 32-bit elements; how exact they have to be, the bound alone decides.
No kernel may reach another device: no remote copies, remote signals or barrier semaphores. Data moves between devices by JAX's collectives and lax.ppermute only.
A program may use at most 64 MiB of HBM per device.

```python
import math
import jax
import jax.numpy as jnp
from jax import lax

NB = 128
RB = 2
PANELS = 2
MB = 16
CB = 4
NT = 2048


def draw_a_matrix(key, part):
    total = MB * NB
    row_groups = MB // RB
    col_groups = MB // CB
    base = jnp.clip(jax.random.normal(key, (total, total), jnp.float32), -6.0, 6.0)
    symmetric = 0.5 * (base + base.T)
    return symmetric.reshape(RB, row_groups, NB, CB, col_groups, NB)


def draw_linv(key, part):
    first_key = jax.random.fold_in(key, 11)
    second_key = jax.random.fold_in(key, 13)
    diagonal = jax.random.uniform(first_key, (PANELS, NB), jnp.float32, 0.8, 1.6)
    entries = jnp.clip(jax.random.normal(second_key, (PANELS, NB, NB), jnp.float32), -3.0, 3.0) * (0.5 / math.sqrt(NB))
    row_index = lax.broadcasted_iota(jnp.int32, (NB, NB), 0)
    col_index = lax.broadcasted_iota(jnp.int32, (NB, NB), 1)
    strict = (row_index > col_index)[None, :, :]
    on_diagonal = (row_index == col_index)[None, :, :]
    zero_value = jnp.zeros((), jnp.float32)
    return jnp.where(strict, entries, zero_value) + jnp.where(on_diagonal, diagonal[:, :, None], zero_value)


def block_levels(rng, extent, cuts, smallest, top_value):
    loudness = 1.0
    for position, shards_of in cuts:
        steps = jax.random.uniform(jax.random.fold_in(jax.random.fold_in(rng, 6), position), (shards_of,), jnp.float32, smallest / len(cuts), top_value / len(cuts))
        loudness = loudness * jnp.repeat(jnp.exp(steps), extent[position] // shards_of).reshape((-1,) + (1,) * (len(extent) - 1 - position))
    return loudness


def gaussian(rng, shape, spread, bound, cuts=(), held_as=jnp.bfloat16):
    drawn = jax.random.normal(rng, shape, jnp.float32) * spread
    if len(cuts) > 0:
        drawn = block_levels(rng, shape, cuts, -0.22, 0.18) * drawn
    return jnp.clip(drawn, min=-bound, max=bound).astype(held_as)


def setup_inputs(seed: int = 0) -> dict:
    key_list = jax.random.split(jax.random.key(seed), 4)
    return {
        "a_matrix": draw_a_matrix(jax.random.fold_in(key_list[3], 71), 0),
        "l_panels": gaussian(key_list[1], (RB, MB // RB, NB, PANELS * NB), (NT // 4) ** -0.5, 0.25, ((1, 8),), jnp.float32),
        "linv": draw_linv(jax.random.fold_in(key_list[3], 71), 0),
    }


def reference(a_matrix, l_panels, linv):
    precise = lax.Precision.HIGHEST
    total = a_matrix.shape[0] * a_matrix.shape[1] * a_matrix.shape[2]
    matrix = a_matrix.reshape(total, total)
    factor = l_panels.reshape(total, PANELS * NB)
    block_ids = jnp.arange(total, dtype=jnp.int32) // NB
    for panel_index in range(PANELS):
        start = panel_index * NB
        inverse = linv[panel_index]
        lower_part = jnp.where((block_ids > panel_index)[:, None], factor[:, start:start + NB], jnp.zeros((), factor.dtype))
        new_rows = jnp.dot(inverse, matrix[start:start + NB, :], precision=precise)
        matrix = matrix - jnp.dot(lower_part, new_rows, precision=precise)
        matrix = matrix.at[start:start + NB, :].set(new_rows)
        new_cols = jnp.dot(matrix[:, start:start + NB], inverse.T, precision=precise)
        matrix = matrix - jnp.dot(new_cols, lower_part.T, precision=precise)
        matrix = matrix.at[:, start:start + NB].set(new_cols)
    return matrix.reshape(a_matrix.shape)
```

```python
import jax
import jax.numpy as jnp
from jax import lax
from jax.sharding import PartitionSpec as P

precise = lax.Precision.HIGHEST
AXES = ("row", "col")


def mm(left, right):
    return jnp.dot(left, right, precision=precise)


def times_transposed(left, right):
    return lax.dot_general(left, right, (((1,), (1,)), ((), ())), precision=precise)


def group_pairs(pairs):
    rounds = []
    for source, target in pairs:
        for entry in rounds:
            if source not in entry[1] and target not in entry[2]:
                entry[0].append((source, target))
                entry[1].add(source)
                entry[2].add(target)
                break
        else:
            rounds.append(([(source, target)], {source}, {target}))
    return [entry[0] for entry in rounds]


def deliver(value, pairs, col_count):
    flat = [(s[0] * col_count + s[1], t[0] * col_count + t[1]) for s, t in pairs]
    total = jnp.zeros_like(value)
    for perm in group_pairs(flat):
        total = total + lax.ppermute(value, AXES, perm)
    return total


def chip_pairs(sources, row_count, col_count):
    chips = row_count // 2
    pairs = []
    for step in range(chips - 1):
        for col in range(col_count):
            src = sources[col]
            others = [k for k in range(chips) if k != src // 2]
            pairs.append(((src, col), (2 * others[step] + src % 2, col)))
    return pairs


def from_two_cores(payload, row_id, row_count, col_count):
    pairs = chip_pairs([0] * col_count, row_count, col_count)
    pairs += chip_pairs([1] * col_count, row_count, col_count)
    held = jnp.where(row_id < 2, payload, deliver(payload, pairs, col_count))
    mate = lax.ppermute(held, "row", [(i, i ^ 1) for i in range(row_count)])
    even = row_id % 2 == 0
    return jnp.where(even, held, mate), jnp.where(even, mate, held)


def per_device(a_matrix, l_panels, linv):
    row_count = lax.axis_size("row")
    col_count = lax.axis_size("col")
    row_id = lax.axis_index("row")
    col_id = lax.axis_index("col")
    row_blocks = a_matrix.shape[0]
    col_blocks = a_matrix.shape[3]
    nb = a_matrix.shape[2]
    ratio = row_count // col_count
    a_loc = a_matrix.reshape(row_blocks * nb, col_blocks * nb)
    l_loc = l_panels.reshape(row_blocks * nb, 2 * nb)
    width = col_blocks * nb

    payload = jnp.concatenate([a_loc[:nb, :], l_loc[:nb, :nb]], 1)
    top0, top1 = from_two_cores(payload, row_id, row_count, col_count)
    b_cols = jnp.concatenate([top0[:, :width], top1[:, :width]], 0)
    link = top1[:, width:]

    halves = []
    for h in range(2):
        pairs = [
            ((rr, h), (rr, cc))
            for cc in range(col_count)
            if cc != h
            for rr in range(row_count)
        ]
        piece = a_loc[:, :nb]
        halves.append(jnp.where(col_id == h, piece, deliver(piece, pairs, col_count)))
    z_rows = jnp.concatenate(halves, 1)

    d_parts = []
    for h in range(2):
        pairs = [((i, h), (i, cc)) for cc in range(col_count) if cc != h for i in range(2)]
        piece = a_loc[:nb, :nb]
        d_parts.append(jnp.where(col_id == h, piece, deliver(piece, pairs, col_count)))
    d0, d1 = from_two_cores(jnp.concatenate(d_parts, 1), row_id, row_count, col_count)
    d_top = jnp.concatenate([d0, d1], 0)

    sources = []
    for i in range(min(ratio, col_blocks)):
        src_rows = [col + i * col_count for col in range(col_count)]
        pairs = chip_pairs(src_rows, row_count, col_count)
        src_id = col_id + i * col_count
        held = jnp.where(row_id == src_id, l_loc, deliver(l_loc, pairs, col_count))
        swap = []
        for col in range(col_count):
            parity = src_rows[col] % 2
            for k in range(row_count // 2):
                swap.append(((2 * k + parity, col), (2 * k + 1 - parity, col)))
        mate = deliver(held, swap, col_count)
        sources.append(jnp.where(row_id % 2 == src_id % 2, held, mate))
    l_cols = jnp.concatenate(
        [sources[k % ratio][(k // ratio) * nb : (k // ratio + 1) * nb] for k in range(col_blocks)],
        0,
    )

    first_inverse = linv[0]
    second_inverse = linv[1]
    corner = -mm(second_inverse, mm(link, first_inverse))
    zero_block = jnp.zeros_like(first_inverse)
    k_top = jnp.concatenate(
        [
            jnp.concatenate([first_inverse, zero_block], 1),
            jnp.concatenate([corner, second_inverse], 1),
        ],
        0,
    )
    k_minus = k_top - jnp.eye(2 * nb, dtype=k_top.dtype)

    def u_rows(factor_rows, first_block):
        u = -mm(factor_rows, k_top)
        head = jnp.where(
            first_block == 0,
            k_minus[:nb],
            jnp.where(first_block == 1, k_minus[nb:], u[:nb]),
        )
        return jnp.concatenate([head, u[nb:]], 0)

    u_i = u_rows(l_loc, row_id)
    u_j = u_rows(l_cols, col_id)
    w_i = z_rows + mm(u_i, d_top)
    out = a_loc + mm(u_i, b_cols) + times_transposed(w_i, u_j)
    return out.reshape(a_matrix.shape)


def solution(mesh):
    in_specs = (P(None, "row", None, None, "col", None), P(None, "row", None, None), P())
    out_specs = P(None, "row", None, None, "col", None)
    return jax.shard_map(
        per_device, mesh=mesh, in_specs=in_specs, out_specs=out_specs, check_vma=False
    )
```

```python
import jax
import jax.numpy as jnp
from jax import lax
from jax.sharding import PartitionSpec as P

precise = lax.Precision.HIGHEST
AXES = ("row", "col")


def mm(left, right):
    return jnp.dot(left, right, precision=precise)


def times_transposed(left, right):
    return lax.dot_general(left, right, (((1,), (1,)), ((), ())), precision=precise)


def flat_permute(value, pairs, col_count):
    flat = [(s[0] * col_count + s[1], t[0] * col_count + t[1]) for s, t in pairs]
    return lax.ppermute(value, AXES, flat)


def cube_rounds(source_chip, bits):
    holders = [source_chip]
    rounds = []
    for bit in bits:
        step = [(h, h ^ (1 << bit)) for h in holders]
        holders = holders + [t for _, t in step]
        rounds.append(step)
    return rounds


def chip_bits(row_count):
    chips = row_count // 2
    count = chips.bit_length() - 1
    assert 1 << count == chips
    return list(range(count))


def from_two_cores(payload, row_id, row_count):
    bits = chip_bits(row_count)
    lanes = [cube_rounds(0, bits), cube_rounds(0, bits[::-1])]
    held = jnp.where(row_id < 2, payload, jnp.zeros_like(payload))
    for step in range(len(bits)):
        perm = [
            (2 * s + core, 2 * t + core)
            for core in range(2)
            for s, t in lanes[core][step]
        ]
        held = held + lax.ppermute(held, "row", perm)
    mate = lax.ppermute(held, "row", [(i, i ^ 1) for i in range(row_count)])
    even = row_id % 2 == 0
    return jnp.where(even, held, mate), jnp.where(even, mate, held)


def factor_sources(l_loc, row_id, col_id, row_count, col_count):
    bits = chip_bits(row_count)
    plan = []
    for col in range(col_count):
        first, second = col, col + col_count
        k1, k2 = first // 2, second // 2
        split = ((k1 ^ k2) & -(k1 ^ k2)).bit_length() - 1
        others = [b for b in bits if b != split]
        plan.append((first % 2, k1, k2, split, cube_rounds(k1, others), cube_rounds(k2, others)))
    is_source = (row_id == col_id) | (row_id == col_id + col_count)
    held = jnp.where(is_source, l_loc, jnp.zeros_like(l_loc))
    for step in range(len(bits) - 1):
        pairs = []
        for col, (lane, _, _, _, rounds1, rounds2) in enumerate(plan):
            for s, t in rounds1[step] + rounds2[step]:
                pairs.append(((2 * s + lane, col), (2 * t + lane, col)))
        held = held + flat_permute(held, pairs, col_count)
    pairs = []
    for col, (lane, _, _, split, _, _) in enumerate(plan):
        for h in range(row_count // 2):
            pairs.append(((2 * h + lane, col), (2 * (h ^ (1 << split)) + lane, col)))
    other = flat_permute(held, pairs, col_count)
    split_of = jnp.array([p[3] for p in plan], jnp.int32)[col_id]
    first_side = jnp.array([p[1] for p in plan], jnp.int32)[col_id]
    in_first = ((row_id // 2) >> split_of) % 2 == (first_side >> split_of) % 2
    both = jnp.concatenate(
        [jnp.where(in_first, held, other), jnp.where(in_first, other, held)], 0
    )
    pairs = []
    for col, (lane, _, _, _, _, _) in enumerate(plan):
        for h in range(row_count // 2):
            pairs.append(((2 * h + lane, col), (2 * h + 1 - lane, col)))
    mate = flat_permute(both, pairs, col_count)
    mine = row_id % 2 == col_id % 2
    return jnp.where(mine, both, mate)


def per_device(a_matrix, l_panels, linv):
    row_count = lax.axis_size("row")
    col_count = lax.axis_size("col")
    row_id = lax.axis_index("row")
    col_id = lax.axis_index("col")
    row_blocks = a_matrix.shape[0]
    col_blocks = a_matrix.shape[3]
    nb = a_matrix.shape[2]
    ratio = row_count // col_count
    assert ratio == 2 and row_count == ratio * col_count
    a_loc = a_matrix.reshape(row_blocks * nb, col_blocks * nb)
    l_loc = l_panels.reshape(row_blocks * nb, 2 * nb)
    width = col_blocks * nb

    piece = a_loc[:, :nb]
    half0 = jnp.where(col_id == 0, piece, jnp.zeros_like(piece))
    half1 = jnp.where(col_id == 1, piece, jnp.zeros_like(piece))
    for shift in range(1, col_count):
        perm = [(h, (h + shift) % col_count) for h in range(2)]
        got = lax.ppermute(piece, "col", perm)
        half0 = jnp.where(col_id == shift, got, half0)
        half1 = jnp.where(col_id == (1 + shift) % col_count, got, half1)
    z_rows = jnp.concatenate([half0, half1], 1)

    payload = jnp.concatenate([a_loc[:nb, :], l_loc[:nb, :nb]], 1)
    top0, top1 = from_two_cores(payload, row_id, row_count)
    b_cols = jnp.concatenate([top0[:, :width], top1[:, :width]], 0)
    link = top1[:, width:]

    d0, d1 = from_two_cores(z_rows[:nb], row_id, row_count)
    d_top = jnp.concatenate([d0, d1], 0)

    both = factor_sources(l_loc, row_id, col_id, row_count, col_count)
    l_cols = jnp.concatenate(
        [both[(k % ratio) * 2 * nb + (k // ratio) * nb :][:nb] for k in range(col_blocks)],
        0,
    )

    first_inverse = linv[0]
    second_inverse = linv[1]
    corner = -mm(second_inverse, mm(link, first_inverse))
    zero_block = jnp.zeros_like(first_inverse)
    k_top = jnp.concatenate(
        [
            jnp.concatenate([first_inverse, zero_block], 1),
            jnp.concatenate([corner, second_inverse], 1),
        ],
        0,
    )
    k_minus = k_top - jnp.eye(2 * nb, dtype=k_top.dtype)

    def u_rows(factor_rows, first_block):
        u = -mm(factor_rows, k_top)
        head = jnp.where(
            first_block == 0,
            k_minus[:nb],
            jnp.where(first_block == 1, k_minus[nb:], u[:nb]),
        )
        return jnp.concatenate([head, u[nb:]], 0)

    u_i = u_rows(l_loc, row_id)
    u_j = u_rows(l_cols, col_id)
    w_i = z_rows + mm(u_i, d_top)
    out = a_loc + mm(u_i, b_cols) + times_transposed(w_i, u_j)
    return out.reshape(a_matrix.shape)


def solution(mesh):
    in_specs = (P(None, "row", None, None, "col", None), P(None, "row", None, None), P())
    out_specs = P(None, "row", None, None, "col", None)
    return jax.shard_map(
        per_device, mesh=mesh, in_specs=in_specs, out_specs=out_specs, check_vma=False
    )
```

```python
import jax
import jax.numpy as jnp
from jax import lax
from jax.sharding import PartitionSpec as P

precise = lax.Precision.HIGHEST
AXES = ("row", "col")


def mm(left, right):
    return jnp.dot(left, right, precision=precise)


def times_transposed(left, right):
    return lax.dot_general(left, right, (((1,), (1,)), ((), ())), precision=precise)


def flat_permute(value, pairs, col_count):
    flat = [(s[0] * col_count + s[1], t[0] * col_count + t[1]) for s, t in pairs]
    return lax.ppermute(value, AXES, flat)


def cube_rounds(source_chip, bits):
    holders = [source_chip]
    rounds = []
    for bit in bits:
        step = [(h, h ^ (1 << bit)) for h in holders]
        holders = holders + [t for _, t in step]
        rounds.append(step)
    return rounds


def chip_bits(row_count):
    chips = row_count // 2
    count = chips.bit_length() - 1
    assert 1 << count == chips
    return list(range(count))


def from_two_cores(payload, row_id, row_count):
    bits = chip_bits(row_count)
    lanes = [cube_rounds(0, bits), cube_rounds(0, bits[::-1])]
    held = jnp.where(row_id < 2, payload, jnp.zeros_like(payload))
    for step in range(len(bits)):
        perm = [
            (2 * s + core, 2 * t + core)
            for core in range(2)
            for s, t in lanes[core][step]
        ]
        held = held + lax.ppermute(held, "row", perm)
    mate = lax.ppermute(held, "row", [(i, i ^ 1) for i in range(row_count)])
    even = row_id % 2 == 0
    return jnp.where(even, held, mate), jnp.where(even, mate, held)


def rows_and_factor(a_part, l_loc, row_id, col_id, row_count, col_count):
    bits = chip_bits(row_count)
    last = bits[-1]
    a_rounds, l_rounds, l_lanes = [], [], []
    for col in range(col_count):
        lane = col % 2
        k1, k2 = col // 2, (col + col_count) // 2
        assert k1 ^ k2 == 1 << last
        a_rounds.append([cube_rounds(0, bits), cube_rounds(0, bits[::-1])])
        l_lanes.append(lane)
        held_chips = [k1, k2]
        steps = []
        for bit in bits:
            steps.append([(h, h ^ (1 << bit)) for h in held_chips])
            held_chips = held_chips + [h ^ (1 << bit) for h in held_chips]
        l_rounds.append(steps)
    nb = a_part.shape[0]
    l_flat = l_loc.reshape(nb, -1)
    is_source = (row_id == col_id) | (row_id == col_id + col_count)
    held = jnp.concatenate(
        [
            jnp.where(row_id < 2, a_part, jnp.zeros_like(a_part)),
            jnp.where(is_source, l_flat, jnp.zeros_like(l_flat)),
        ],
        1,
    )
    split = a_part.shape[1]
    other = None
    for step in range(len(bits)):
        pairs = set()
        for col in range(col_count):
            lane = l_lanes[col]
            for s, t in a_rounds[col][0][step] + l_rounds[col][step]:
                pairs.add(((2 * s + lane, col), (2 * t + lane, col)))
            for s, t in a_rounds[col][1][step]:
                pairs.add(((2 * s + 1 - lane, col), (2 * t + 1 - lane, col)))
        got = flat_permute(held, sorted(pairs), col_count)
        if step < len(bits) - 1:
            held = held + got
        else:
            other = got[:, split:]
            held = jnp.concatenate([held[:, :split] + got[:, :split], held[:, split:]], 1)
    a_held = held[:, :split]
    a_mate = lax.ppermute(a_held, "row", [(i, i ^ 1) for i in range(row_count)])
    even = row_id % 2 == 0
    top0 = jnp.where(even, a_held, a_mate)
    top1 = jnp.where(even, a_mate, a_held)
    first_chip = col_id // 2
    in_first = ((row_id // 2) >> last) % 2 == (first_chip >> last) % 2
    mine = held[:, split:].reshape(l_loc.shape)
    theirs = other.reshape(l_loc.shape)
    both = jnp.concatenate(
        [jnp.where(in_first, mine, theirs), jnp.where(in_first, theirs, mine)], 0
    )
    pairs = []
    for col in range(col_count):
        lane = l_lanes[col]
        for h in range(row_count // 2):
            pairs.append(((2 * h + lane, col), (2 * h + 1 - lane, col)))
    mate = flat_permute(both, pairs, col_count)
    return top0, top1, jnp.where(row_id % 2 == col_id % 2, both, mate)


def per_device(a_matrix, l_panels, linv):
    row_count = lax.axis_size("row")
    col_count = lax.axis_size("col")
    row_id = lax.axis_index("row")
    col_id = lax.axis_index("col")
    row_blocks = a_matrix.shape[0]
    col_blocks = a_matrix.shape[3]
    nb = a_matrix.shape[2]
    ratio = row_count // col_count
    assert ratio == 2 and row_count == ratio * col_count
    a_loc = a_matrix.reshape(row_blocks * nb, col_blocks * nb)
    l_loc = l_panels.reshape(row_blocks * nb, 2 * nb)
    width = col_blocks * nb

    piece = a_loc[:, :nb]
    half0 = jnp.where(col_id == 0, piece, jnp.zeros_like(piece))
    half1 = jnp.where(col_id == 1, piece, jnp.zeros_like(piece))
    for shift in range(1, col_count):
        perm = [(h, (h + shift) % col_count) for h in range(2)]
        got = lax.ppermute(piece, "col", perm)
        half0 = jnp.where(col_id == shift, got, half0)
        half1 = jnp.where(col_id == (1 + shift) % col_count, got, half1)
    z_rows = jnp.concatenate([half0, half1], 1)

    payload = jnp.concatenate([a_loc[:nb, :], l_loc[:nb, :nb]], 1)
    top0, top1, both = rows_and_factor(payload, l_loc, row_id, col_id, row_count, col_count)
    b_cols = jnp.concatenate([top0[:, :width], top1[:, :width]], 0)
    link = top1[:, width:]

    d0, d1 = from_two_cores(z_rows[:nb], row_id, row_count)
    d_top = jnp.concatenate([d0, d1], 0)

    l_cols = jnp.concatenate(
        [both[(k % ratio) * 2 * nb + (k // ratio) * nb :][:nb] for k in range(col_blocks)],
        0,
    )

    first_inverse = linv[0]
    second_inverse = linv[1]
    corner = -mm(second_inverse, mm(link, first_inverse))
    zero_block = jnp.zeros_like(first_inverse)
    k_top = jnp.concatenate(
        [
            jnp.concatenate([first_inverse, zero_block], 1),
            jnp.concatenate([corner, second_inverse], 1),
        ],
        0,
    )
    k_minus = k_top - jnp.eye(2 * nb, dtype=k_top.dtype)

    def u_rows(factor_rows, first_block):
        u = -mm(factor_rows, k_top)
        head = jnp.where(
            first_block == 0,
            k_minus[:nb],
            jnp.where(first_block == 1, k_minus[nb:], u[:nb]),
        )
        return jnp.concatenate([head, u[nb:]], 0)

    u_i = u_rows(l_loc, row_id)
    u_j = u_rows(l_cols, col_id)
    w_i = z_rows + mm(u_i, d_top)
    out = a_loc + mm(u_i, b_cols) + times_transposed(w_i, u_j)
    return out.reshape(a_matrix.shape)


def solution(mesh):
    in_specs = (P(None, "row", None, None, "col", None), P(None, "row", None, None), P())
    out_specs = P(None, "row", None, None, "col", None)
    return jax.shard_map(
        per_device, mesh=mesh, in_specs=in_specs, out_specs=out_specs, check_vma=False
    )
```

```python
import jax
import jax.numpy as jnp
from jax import lax
from jax.sharding import PartitionSpec as P

precise = lax.Precision.HIGHEST
AXES = ("row", "col")


def mm(left, right):
    return jnp.dot(left, right, precision=precise)


def times_transposed(left, right):
    return lax.dot_general(left, right, (((1,), (1,)), ((), ())), precision=precise)


def flat_permute(value, pairs, col_count):
    flat = [(s[0] * col_count + s[1], t[0] * col_count + t[1]) for s, t in pairs]
    return lax.ppermute(value, AXES, flat)


def cube_rounds(source_chip, bits):
    holders = [source_chip]
    rounds = []
    for bit in bits:
        step = [(h, h ^ (1 << bit)) for h in holders]
        holders = holders + [t for _, t in step]
        rounds.append(step)
    return rounds


def chip_bits(row_count):
    chips = row_count // 2
    count = chips.bit_length() - 1
    assert 1 << count == chips
    return list(range(count))


def from_two_cores(payload, row_id, row_count):
    bits = chip_bits(row_count)
    lanes = [cube_rounds(0, bits), cube_rounds(0, bits[::-1])]
    held = jnp.where(row_id < 2, payload, jnp.zeros_like(payload))
    for step in range(len(bits)):
        perm = [
            (2 * s + core, 2 * t + core)
            for core in range(2)
            for s, t in lanes[core][step]
        ]
        held = held + lax.ppermute(held, "row", perm)
    mate = lax.ppermute(held, "row", [(i, i ^ 1) for i in range(row_count)])
    even = row_id % 2 == 0
    return jnp.where(even, held, mate), jnp.where(even, mate, held)


def factor_sources(l_loc, row_id, col_id, row_count, col_count):
    bits = chip_bits(row_count)
    plan = []
    for col in range(col_count):
        first, second = col, col + col_count
        k1, k2 = first // 2, second // 2
        split = ((k1 ^ k2) & -(k1 ^ k2)).bit_length() - 1
        others = [b for b in bits if b != split]
        plan.append((first % 2, k1, k2, split, cube_rounds(k1, others), cube_rounds(k2, others)))
    is_source = (row_id == col_id) | (row_id == col_id + col_count)
    held = jnp.where(is_source, l_loc, jnp.zeros_like(l_loc))
    for step in range(len(bits) - 1):
        pairs = []
        for col, (lane, _, _, _, rounds1, rounds2) in enumerate(plan):
            for s, t in rounds1[step] + rounds2[step]:
                pairs.append(((2 * s + lane, col), (2 * t + lane, col)))
        held = held + flat_permute(held, pairs, col_count)
    pairs = []
    for col, (lane, _, _, split, _, _) in enumerate(plan):
        for h in range(row_count // 2):
            pairs.append(((2 * h + lane, col), (2 * (h ^ (1 << split)) + lane, col)))
    other = flat_permute(held, pairs, col_count)
    split_of = jnp.array([p[3] for p in plan], jnp.int32)[col_id]
    first_side = jnp.array([p[1] for p in plan], jnp.int32)[col_id]
    in_first = ((row_id // 2) >> split_of) % 2 == (first_side >> split_of) % 2
    both = jnp.concatenate(
        [jnp.where(in_first, held, other), jnp.where(in_first, other, held)], 0
    )
    pairs = []
    for col, (lane, _, _, _, _, _) in enumerate(plan):
        for h in range(row_count // 2):
            pairs.append(((2 * h + lane, col), (2 * h + 1 - lane, col)))
    mate = flat_permute(both, pairs, col_count)
    mine = row_id % 2 == col_id % 2
    return jnp.where(mine, both, mate)


def per_device(a_matrix, l_panels, linv):
    row_count = lax.axis_size("row")
    col_count = lax.axis_size("col")
    row_id = lax.axis_index("row")
    col_id = lax.axis_index("col")
    row_blocks = a_matrix.shape[0]
    col_blocks = a_matrix.shape[3]
    nb = a_matrix.shape[2]
    ratio = row_count // col_count
    assert ratio == 2 and row_count == ratio * col_count
    a_loc = a_matrix.reshape(row_blocks * nb, col_blocks * nb)
    l_loc = l_panels.reshape(row_blocks * nb, 2 * nb)
    width = col_blocks * nb

    payload = jnp.concatenate([a_loc[:nb, :], l_loc[:nb, :nb]], 1)
    top0, top1 = from_two_cores(payload, row_id, row_count)
    b_cols = jnp.concatenate([top0[:, :width], top1[:, :width]], 0)
    link = top1[:, width:]

    both = factor_sources(l_loc, row_id, col_id, row_count, col_count)
    l_cols = jnp.concatenate(
        [both[(k % ratio) * 2 * nb + (k // ratio) * nb :][:nb] for k in range(col_blocks)],
        0,
    )

    first_inverse = linv[0]
    second_inverse = linv[1]
    corner = -mm(second_inverse, mm(link, first_inverse))
    zero_block = jnp.zeros_like(first_inverse)
    k_top = jnp.concatenate(
        [
            jnp.concatenate([first_inverse, zero_block], 1),
            jnp.concatenate([corner, second_inverse], 1),
        ],
        0,
    )
    k_minus = k_top - jnp.eye(2 * nb, dtype=k_top.dtype)

    def u_rows(factor_rows, first_block):
        u = -mm(factor_rows, k_top)
        head = jnp.where(
            first_block == 0,
            k_minus[:nb],
            jnp.where(first_block == 1, k_minus[nb:], u[:nb]),
        )
        return jnp.concatenate([head, u[nb:]], 0)

    u_i = u_rows(l_loc, row_id)
    u_j = u_rows(l_cols, col_id)

    piece = a_loc[:, :nb] + mm(u_i, b_cols[:, :nb])
    half0 = jnp.where(col_id == 0, piece, jnp.zeros_like(piece))
    half1 = jnp.where(col_id == 1, piece, jnp.zeros_like(piece))
    for shift in range(1, col_count):
        perm = [(h, (h + shift) % col_count) for h in range(2)]
        got = lax.ppermute(piece, "col", perm)
        half0 = jnp.where(col_id == shift, got, half0)
        half1 = jnp.where(col_id == (1 + shift) % col_count, got, half1)
    w_i = jnp.concatenate([half0, half1], 1)
    out = a_loc + mm(u_i, b_cols) + times_transposed(w_i, u_j)
    return out.reshape(a_matrix.shape)


def solution(mesh):
    in_specs = (P(None, "row", None, None, "col", None), P(None, "row", None, None), P())
    out_specs = P(None, "row", None, None, "col", None)
    return jax.shard_map(
        per_device, mesh=mesh, in_specs=in_specs, out_specs=out_specs, check_vma=False
    )
```

```python
import jax
import jax.numpy as jnp
from jax import lax
from jax.sharding import PartitionSpec as P

precise = lax.Precision.HIGHEST
AXES = ("row", "col")


def mm(left, right):
    return jnp.dot(left, right, precision=precise)


def times_transposed(left, right):
    return lax.dot_general(left, right, (((1,), (1,)), ((), ())), precision=precise)


def flat_permute(value, pairs, col_count):
    flat = [(s[0] * col_count + s[1], t[0] * col_count + t[1]) for s, t in pairs]
    return lax.ppermute(value, AXES, flat)


def cube_rounds(source_chip, bits):
    holders = [source_chip]
    rounds = []
    for bit in bits:
        step = [(h, h ^ (1 << bit)) for h in holders]
        holders = holders + [t for _, t in step]
        rounds.append(step)
    return rounds


def chip_bits(row_count):
    chips = row_count // 2
    count = chips.bit_length() - 1
    assert 1 << count == chips
    return list(range(count))


def from_two_cores(payload, row_id, row_count, col_count, planes=None, hold=None):
    planes = range(col_count) if planes is None else planes
    bits = chip_bits(row_count)
    lanes = [cube_rounds(0, bits), cube_rounds(0, bits[::-1])]
    held = jnp.where(row_id < 2, payload, jnp.zeros_like(payload))
    for step in range(len(bits)):
        pairs = [
            ((2 * s + core, col), (2 * t + core, col))
            for col in planes
            for core in range(2)
            for s, t in lanes[core][step]
        ]
        held = held + flat_permute(held, pairs, col_count)
        if step == 0 and hold is not None:
            held, hold = lax.optimization_barrier((held, hold))
    pairs = [((i, col), (i ^ 1, col)) for col in planes for i in range(row_count)]
    mate = flat_permute(held, pairs, col_count)
    even = row_id % 2 == 0
    return jnp.where(even, held, mate), jnp.where(even, mate, held), hold


def factor_sources(l_loc, row_id, col_id, row_count, col_count):
    bits = chip_bits(row_count)
    plan = []
    for col in range(col_count):
        first, second = col, col + col_count
        k1, k2 = first // 2, second // 2
        split = ((k1 ^ k2) & -(k1 ^ k2)).bit_length() - 1
        others = [b for b in bits if b != split]
        plan.append((first % 2, k1, k2, split, cube_rounds(k1, others), cube_rounds(k2, others)))
    is_source = (row_id == col_id) | (row_id == col_id + col_count)
    held = jnp.where(is_source, l_loc, jnp.zeros_like(l_loc))
    for step in range(len(bits) - 1):
        pairs = []
        for col, (lane, _, _, _, rounds1, rounds2) in enumerate(plan):
            for s, t in rounds1[step] + rounds2[step]:
                pairs.append(((2 * s + lane, col), (2 * t + lane, col)))
        held = held + flat_permute(held, pairs, col_count)
    pairs = []
    for col, (lane, _, _, split, _, _) in enumerate(plan):
        for h in range(row_count // 2):
            pairs.append(((2 * h + lane, col), (2 * (h ^ (1 << split)) + lane, col)))
    other = flat_permute(held, pairs, col_count)
    split_of = jnp.array([p[3] for p in plan], jnp.int32)[col_id]
    first_side = jnp.array([p[1] for p in plan], jnp.int32)[col_id]
    in_first = ((row_id // 2) >> split_of) % 2 == (first_side >> split_of) % 2
    both = jnp.concatenate(
        [jnp.where(in_first, held, other), jnp.where(in_first, other, held)], 0
    )
    pairs = []
    for col, (lane, _, _, _, _, _) in enumerate(plan):
        for h in range(row_count // 2):
            pairs.append(((2 * h + lane, col), (2 * h + 1 - lane, col)))
    mate = flat_permute(both, pairs, col_count)
    mine = row_id % 2 == col_id % 2
    return jnp.where(mine, both, mate)


def per_device(a_matrix, l_panels, linv):
    row_count = lax.axis_size("row")
    col_count = lax.axis_size("col")
    row_id = lax.axis_index("row")
    col_id = lax.axis_index("col")
    row_blocks = a_matrix.shape[0]
    col_blocks = a_matrix.shape[3]
    nb = a_matrix.shape[2]
    ratio = row_count // col_count
    assert ratio == 2 and row_count == ratio * col_count
    a_loc = a_matrix.reshape(row_blocks * nb, col_blocks * nb)
    l_loc = l_panels.reshape(row_blocks * nb, 2 * nb)
    width = col_blocks * nb

    quick = jnp.concatenate([a_loc[:nb, :nb], l_loc[:nb, :nb]], 1)
    quick0, quick1, _ = from_two_cores(quick, row_id, row_count, col_count, planes=range(2))
    d_cols = jnp.concatenate([quick0[:, :nb], quick1[:, :nb]], 0)
    quick_link = quick1[:, nb:]

    both = factor_sources(l_loc, row_id, col_id, row_count, col_count)
    l_cols = jnp.concatenate(
        [both[(k % ratio) * 2 * nb + (k // ratio) * nb :][:nb] for k in range(col_blocks)],
        0,
    )

    first_inverse = linv[0]
    second_inverse = linv[1]
    zero_block = jnp.zeros_like(first_inverse)

    def top_of_m(link_block):
        corner = -mm(second_inverse, mm(link_block, first_inverse))
        return jnp.concatenate(
            [
                jnp.concatenate([first_inverse, zero_block], 1),
                jnp.concatenate([corner, second_inverse], 1),
            ],
            0,
        )

    def u_rows(factor_rows, first_block, k_top):
        k_minus = k_top - jnp.eye(2 * nb, dtype=k_top.dtype)
        u = -mm(factor_rows, k_top)
        head = jnp.where(
            first_block == 0,
            k_minus[:nb],
            jnp.where(first_block == 1, k_minus[nb:], u[:nb]),
        )
        return jnp.concatenate([head, u[nb:]], 0)

    k_quick = top_of_m(quick_link)
    u_quick = u_rows(l_loc, row_id, k_quick)
    piece = a_loc[:, :nb] + mm(u_quick, d_cols)
    half0 = jnp.where(col_id == 0, piece, jnp.zeros_like(piece))
    half1 = jnp.where(col_id == 1, piece, jnp.zeros_like(piece))
    payload = jnp.concatenate([a_loc[:nb, :], l_loc[:nb, :nb]], 1)
    top0, top1, piece = from_two_cores(payload, row_id, row_count, col_count, hold=piece)
    b_cols = jnp.concatenate([top0[:, :width], top1[:, :width]], 0)
    link = jnp.where(col_id < 2, quick_link, top1[:, width:])
    k_top = top_of_m(link)
    u_i = u_rows(l_loc, row_id, k_top)
    u_j = u_rows(l_cols, col_id, k_top)
    for shift in range(1, col_count):
        perm = [(h, (h + shift) % col_count) for h in range(2)]
        got = lax.ppermute(piece, "col", perm)
        half0 = jnp.where(col_id == shift, got, half0)
        half1 = jnp.where(col_id == (1 + shift) % col_count, got, half1)
    w_i = jnp.concatenate([half0, half1], 1)
    out = a_loc + mm(u_i, b_cols) + times_transposed(w_i, u_j)
    return out.reshape(a_matrix.shape)


def solution(mesh):
    in_specs = (P(None, "row", None, None, "col", None), P(None, "row", None, None), P())
    out_specs = P(None, "row", None, None, "col", None)
    return jax.shard_map(
        per_device, mesh=mesh, in_specs=in_specs, out_specs=out_specs, check_vma=False
    )
```

```python
import jax
import jax.numpy as jnp
from jax import lax
from jax.sharding import PartitionSpec as P

precise = lax.Precision.HIGHEST
AXES = ("row", "col")


def mm(left, right):
    return jnp.dot(left, right, precision=precise)


def times_transposed(left, right):
    return lax.dot_general(left, right, (((1,), (1,)), ((), ())), precision=precise)


def flat_permute(value, pairs, col_count):
    flat = [(s[0] * col_count + s[1], t[0] * col_count + t[1]) for s, t in pairs]
    return lax.ppermute(value, AXES, flat)


def cube_rounds(source_chip, bits):
    holders = [source_chip]
    rounds = []
    for bit in bits:
        step = [(h, h ^ (1 << bit)) for h in holders]
        holders = holders + [t for _, t in step]
        rounds.append(step)
    return rounds


def chip_bits(row_count):
    chips = row_count // 2
    count = chips.bit_length() - 1
    assert 1 << count == chips
    return list(range(count))


def from_two_cores(payload, row_id, row_count):
    bits = chip_bits(row_count)
    lanes = [cube_rounds(0, bits), cube_rounds(0, bits[::-1])]
    held = payload
    for step in range(len(bits)):
        perm = [
            (2 * s + core, 2 * t + core)
            for core in range(2)
            for s, t in lanes[core][step]
        ]
        got = lax.ppermute(held, "row", perm)
        held = jnp.where(row_id < 2, payload, got) if step == 0 else held + got
    mate = lax.ppermute(held, "row", [(i, i ^ 1) for i in range(row_count)])
    even = row_id % 2 == 0
    return jnp.where(even, held, mate), jnp.where(even, mate, held)


def factor_sources(l_loc, row_id, col_id, row_count, col_count):
    bits = chip_bits(row_count)
    plan = []
    for col in range(col_count):
        first, second = col, col + col_count
        k1, k2 = first // 2, second // 2
        split = ((k1 ^ k2) & -(k1 ^ k2)).bit_length() - 1
        others = [b for b in bits if b != split]
        plan.append((first % 2, k1, k2, split, cube_rounds(k1, others), cube_rounds(k2, others)))
    is_source = (row_id == col_id) | (row_id == col_id + col_count)
    held = l_loc
    for step in range(len(bits) - 1):
        pairs = []
        for col, (lane, _, _, _, rounds1, rounds2) in enumerate(plan):
            for s, t in rounds1[step] + rounds2[step]:
                pairs.append(((2 * s + lane, col), (2 * t + lane, col)))
        got = flat_permute(held, pairs, col_count)
        held = jnp.where(is_source, l_loc, got) if step == 0 else held + got
    pairs = []
    for col, (lane, _, _, split, _, _) in enumerate(plan):
        for h in range(row_count // 2):
            pairs.append(((2 * h + lane, col), (2 * (h ^ (1 << split)) + lane, col)))
    other = flat_permute(held, pairs, col_count)
    split_of = jnp.array([p[3] for p in plan], jnp.int32)[col_id]
    first_side = jnp.array([p[1] for p in plan], jnp.int32)[col_id]
    in_first = ((row_id // 2) >> split_of) % 2 == (first_side >> split_of) % 2
    both = jnp.concatenate(
        [jnp.where(in_first, held, other), jnp.where(in_first, other, held)], 0
    )
    pairs = []
    for col, (lane, _, _, _, _, _) in enumerate(plan):
        for h in range(row_count // 2):
            pairs.append(((2 * h + lane, col), (2 * h + 1 - lane, col)))
    mate = flat_permute(both, pairs, col_count)
    mine = row_id % 2 == col_id % 2
    return jnp.where(mine, both, mate)


def per_device(a_matrix, l_panels, linv):
    row_count = lax.axis_size("row")
    col_count = lax.axis_size("col")
    row_id = lax.axis_index("row")
    col_id = lax.axis_index("col")
    row_blocks = a_matrix.shape[0]
    col_blocks = a_matrix.shape[3]
    nb = a_matrix.shape[2]
    ratio = row_count // col_count
    assert ratio == 2 and row_count == ratio * col_count
    a_loc = a_matrix.reshape(row_blocks * nb, col_blocks * nb)
    l_loc = l_panels.reshape(row_blocks * nb, 2 * nb)
    width = col_blocks * nb

    top_rows = a_matrix[0].reshape(nb * col_blocks, nb)
    payload = jnp.concatenate([top_rows, l_panels[0, 0, :, :nb]], 0)
    top0, top1 = from_two_cores(payload, row_id, row_count)
    b_cols = jnp.concatenate(
        [top0[: nb * col_blocks].reshape(nb, width), top1[: nb * col_blocks].reshape(nb, width)], 0
    )
    link = top1[nb * col_blocks :]

    both = factor_sources(l_loc, row_id, col_id, row_count, col_count)
    l_cols = jnp.concatenate(
        [both[(k % ratio) * 2 * nb + (k // ratio) * nb :][:nb] for k in range(col_blocks)],
        0,
    )

    first_inverse = linv[0]
    second_inverse = linv[1]
    corner = -mm(second_inverse, mm(link, first_inverse))
    zero_block = jnp.zeros_like(first_inverse)
    k_top = jnp.concatenate(
        [
            jnp.concatenate([first_inverse, zero_block], 1),
            jnp.concatenate([corner, second_inverse], 1),
        ],
        0,
    )
    k_minus = k_top - jnp.eye(2 * nb, dtype=k_top.dtype)

    def u_rows(factor_rows, first_block):
        u = -mm(factor_rows, k_top)
        head = jnp.where(
            first_block == 0,
            k_minus[:nb],
            jnp.where(first_block == 1, k_minus[nb:], u[:nb]),
        )
        return jnp.concatenate([head, u[nb:]], 0)

    u_i = u_rows(l_loc, row_id)
    u_j = u_rows(l_cols, col_id)

    piece = a_loc[:, :nb] + mm(u_i, b_cols[:, :nb])
    half0 = jnp.where(col_id == 0, piece, jnp.zeros_like(piece))
    half1 = jnp.where(col_id == 1, piece, jnp.zeros_like(piece))
    for shift in range(1, col_count):
        perm = [(h, (h + shift) % col_count) for h in range(2)]
        got = lax.ppermute(piece, "col", perm)
        half0 = jnp.where(col_id == shift, got, half0)
        half1 = jnp.where(col_id == (1 + shift) % col_count, got, half1)
    w_i = jnp.concatenate([half0, half1], 1)
    out = a_loc + mm(u_i, b_cols) + times_transposed(w_i, u_j)
    return out.reshape(a_matrix.shape)


def solution(mesh):
    in_specs = (P(None, "row", None, None, "col", None), P(None, "row", None, None), P())
    out_specs = P(None, "row", None, None, "col", None)
    return jax.shard_map(
        per_device, mesh=mesh, in_specs=in_specs, out_specs=out_specs, check_vma=False
    )
```

```python
import jax
import jax.numpy as jnp
from jax import lax
from jax.sharding import PartitionSpec as P

precise = lax.Precision.HIGHEST
AXES = ("row", "col")


def mm(left, right):
    return jnp.dot(left, right, precision=precise)


def times_transposed(left, right):
    return lax.dot_general(left, right, (((1,), (1,)), ((), ())), precision=precise)


def flat_permute(value, pairs, col_count):
    flat = [(s[0] * col_count + s[1], t[0] * col_count + t[1]) for s, t in pairs]
    return lax.ppermute(value, AXES, flat)


def cube_rounds(source_chip, bits):
    holders = [source_chip]
    rounds = []
    for bit in bits:
        step = [(h, h ^ (1 << bit)) for h in holders]
        holders = holders + [t for _, t in step]
        rounds.append(step)
    return rounds


def chip_bits(row_count):
    chips = row_count // 2
    count = chips.bit_length() - 1
    assert 1 << count == chips
    return list(range(count))


def from_two_cores(payload, row_id, row_count):
    bits = chip_bits(row_count)
    lanes = [cube_rounds(0, bits), cube_rounds(0, bits[::-1])]
    held = payload
    for step in range(len(bits)):
        perm = [
            (2 * s + core, 2 * t + core)
            for core in range(2)
            for s, t in lanes[core][step]
        ]
        got = lax.ppermute(held, "row", perm)
        held = jnp.where(row_id < 2, payload, got) if step == 0 else held + got
    mate = lax.ppermute(held, "row", [(i, i ^ 1) for i in range(row_count)])
    even = row_id % 2 == 0
    return jnp.where(even, held, mate), jnp.where(even, mate, held)


def factor_sources(l_loc, row_id, col_id, row_count, col_count):
    bits = chip_bits(row_count)
    plan = []
    for col in range(col_count):
        first, second = col, col + col_count
        k1, k2 = first // 2, second // 2
        split = ((k1 ^ k2) & -(k1 ^ k2)).bit_length() - 1
        others = [b for b in bits if b != split]
        plan.append((first % 2, k1, k2, split, cube_rounds(k1, others), cube_rounds(k2, others)))
    is_source = (row_id == col_id) | (row_id == col_id + col_count)
    held = l_loc
    for step in range(len(bits) - 1):
        pairs = []
        for col, (lane, _, _, _, rounds1, rounds2) in enumerate(plan):
            for s, t in rounds1[step] + rounds2[step]:
                pairs.append(((2 * s + lane, col), (2 * t + lane, col)))
        got = flat_permute(held, pairs, col_count)
        held = jnp.where(is_source, l_loc, got) if step == 0 else held + got
    pairs = []
    for col, (lane, _, _, split, _, _) in enumerate(plan):
        for h in range(row_count // 2):
            pairs.append(((2 * h + lane, col), (2 * (h ^ (1 << split)) + lane, col)))
    other = flat_permute(held, pairs, col_count)
    split_of = jnp.array([p[3] for p in plan], jnp.int32)[col_id]
    first_side = jnp.array([p[1] for p in plan], jnp.int32)[col_id]
    in_first = ((row_id // 2) >> split_of) % 2 == (first_side >> split_of) % 2
    both = jnp.concatenate(
        [jnp.where(in_first, held, other), jnp.where(in_first, other, held)], 0
    )
    pairs = []
    for col, (lane, _, _, _, _, _) in enumerate(plan):
        for h in range(row_count // 2):
            pairs.append(((2 * h + lane, col), (2 * h + 1 - lane, col)))
    mate = flat_permute(both, pairs, col_count)
    mine = row_id % 2 == col_id % 2
    return jnp.where(mine, both, mate)


def per_device(a_matrix, l_panels, linv):
    row_count = lax.axis_size("row")
    col_count = lax.axis_size("col")
    row_id = lax.axis_index("row")
    col_id = lax.axis_index("col")
    row_blocks = a_matrix.shape[0]
    col_blocks = a_matrix.shape[3]
    nb = a_matrix.shape[2]
    ratio = row_count // col_count
    assert ratio == 2 and row_count == ratio * col_count
    a_loc = a_matrix.reshape(row_blocks * nb, col_blocks * nb)
    l_loc = l_panels.reshape(row_blocks * nb, 2 * nb)
    width = col_blocks * nb

    top_rows = a_matrix[0].reshape(nb * col_blocks, nb)
    payload = jnp.concatenate([top_rows, l_panels[0, 0, :, :nb]], 0)
    top0, top1 = from_two_cores(payload, row_id, row_count)
    b_cols = jnp.concatenate(
        [top0[: nb * col_blocks].reshape(nb, width), top1[: nb * col_blocks].reshape(nb, width)], 0
    )
    link = top1[nb * col_blocks :]

    both = factor_sources(l_loc, row_id, col_id, row_count, col_count)
    l_cols = jnp.concatenate(
        [both[(k % ratio) * 2 * nb + (k // ratio) * nb :][:nb] for k in range(col_blocks)],
        0,
    )

    first_inverse = linv[0]
    second_inverse = linv[1]
    corner = -mm(second_inverse, mm(link, first_inverse))
    zero_block = jnp.zeros_like(first_inverse)
    k_top = jnp.concatenate(
        [
            jnp.concatenate([first_inverse, zero_block], 1),
            jnp.concatenate([corner, second_inverse], 1),
        ],
        0,
    )
    k_minus = k_top - jnp.eye(2 * nb, dtype=k_top.dtype)

    def u_rows(factor_rows, first_block):
        u = -mm(factor_rows, k_top)
        head = jnp.where(
            first_block == 0,
            k_minus[:nb],
            jnp.where(first_block == 1, k_minus[nb:], u[:nb]),
        )
        return jnp.concatenate([head, u[nb:]], 0)

    u_i = u_rows(l_loc, row_id)
    u_j = u_rows(l_cols, col_id)

    piece = a_loc[:, :nb] + mm(u_i, b_cols[:, :nb])
    half0 = jnp.where(col_id == 0, piece, jnp.zeros_like(piece))
    half1 = jnp.where(col_id == 1, piece, jnp.zeros_like(piece))
    for shift in range(1, col_count):
        perm = [(h, (h + shift) % col_count) for h in range(2)]
        send = piece
        if shift == col_count - 1 and col_count >= 4:
            perm = [(1, 0), (col_count - 2, col_count - 1)]
            send = jnp.where(col_id == col_count - 2, half0, piece)
        got = lax.ppermute(send, "col", perm)
        half0 = jnp.where(col_id == shift, got, half0)
        half1 = jnp.where(col_id == (1 + shift) % col_count, got, half1)
    w_i = jnp.concatenate([half0, half1], 1)
    out = a_loc + mm(u_i, b_cols) + times_transposed(w_i, u_j)
    return out.reshape(a_matrix.shape)


def solution(mesh):
    in_specs = (P(None, "row", None, None, "col", None), P(None, "row", None, None), P())
    out_specs = P(None, "row", None, None, "col", None)
    return jax.shard_map(
        per_device, mesh=mesh, in_specs=in_specs, out_specs=out_specs, check_vma=False
    )
```

```python
import jax
import jax.numpy as jnp
from jax import lax
from jax.sharding import PartitionSpec as P

precise = lax.Precision.HIGHEST
AXES = ("row", "col")


def mm(left, right):
    return jnp.dot(left, right, precision=precise)


def times_transposed(left, right):
    return lax.dot_general(left, right, (((1,), (1,)), ((), ())), precision=precise)


def flat_permute(value, pairs, col_count):
    flat = [(s[0] * col_count + s[1], t[0] * col_count + t[1]) for s, t in pairs]
    return lax.ppermute(value, AXES, flat)


def cube_rounds(source_chip, bits):
    holders = [source_chip]
    rounds = []
    for bit in bits:
        step = [(h, h ^ (1 << bit)) for h in holders]
        holders = holders + [t for _, t in step]
        rounds.append(step)
    return rounds


def chip_bits(row_count):
    chips = row_count // 2
    count = chips.bit_length() - 1
    assert 1 << count == chips
    return list(range(count))


def from_two_cores(payload, row_id, row_count):
    bits = chip_bits(row_count)
    lanes = [cube_rounds(0, bits), cube_rounds(0, bits[::-1])]
    held = payload
    for step in range(len(bits)):
        perm = [
            (2 * s + core, 2 * t + core)
            for core in range(2)
            for s, t in lanes[core][step]
        ]
        got = lax.ppermute(held, "row", perm)
        held = jnp.where(row_id < 2, payload, got) if step == 0 else held + got
    mate = lax.ppermute(held, "row", [(i, i ^ 1) for i in range(row_count)])
    even = row_id % 2 == 0
    return jnp.where(even, held, mate), jnp.where(even, mate, held)


def factor_sources(l_loc, row_id, col_id, row_count, col_count):
    bits = chip_bits(row_count)
    plan = []
    for col in range(col_count):
        first, second = col, col + col_count
        k1, k2 = first // 2, second // 2
        split = ((k1 ^ k2) & -(k1 ^ k2)).bit_length() - 1
        others = [b for b in bits if b != split]
        plan.append((first % 2, k1, k2, split, cube_rounds(k1, others), cube_rounds(k2, others)))
    is_source = (row_id == col_id) | (row_id == col_id + col_count)
    held = l_loc
    for step in range(len(bits) - 1):
        pairs = []
        for col, (lane, _, _, _, rounds1, rounds2) in enumerate(plan):
            for s, t in rounds1[step] + rounds2[step]:
                pairs.append(((2 * s + lane, col), (2 * t + lane, col)))
        got = flat_permute(held, pairs, col_count)
        held = jnp.where(is_source, l_loc, got) if step == 0 else held + got
    pairs = []
    for col, (lane, _, _, split, _, _) in enumerate(plan):
        for h in range(row_count // 2):
            pairs.append(((2 * h + lane, col), (2 * (h ^ (1 << split)) + lane, col)))
    other = flat_permute(held, pairs, col_count)
    split_of = jnp.array([p[3] for p in plan], jnp.int32)[col_id]
    first_side = jnp.array([p[1] for p in plan], jnp.int32)[col_id]
    in_first = ((row_id // 2) >> split_of) % 2 == (first_side >> split_of) % 2
    both = jnp.concatenate(
        [jnp.where(in_first, held, other), jnp.where(in_first, other, held)], 0
    )
    pairs = []
    for col, (lane, _, _, _, _, _) in enumerate(plan):
        for h in range(row_count // 2):
            pairs.append(((2 * h + lane, col), (2 * h + 1 - lane, col)))
    mate = flat_permute(both, pairs, col_count)
    mine = row_id % 2 == col_id % 2
    return jnp.where(mine, both, mate)


def per_device(a_matrix, l_panels, linv):
    row_count = lax.axis_size("row")
    col_count = lax.axis_size("col")
    row_id = lax.axis_index("row")
    col_id = lax.axis_index("col")
    row_blocks = a_matrix.shape[0]
    col_blocks = a_matrix.shape[3]
    nb = a_matrix.shape[2]
    ratio = row_count // col_count
    assert ratio == 2 and row_count == ratio * col_count
    a_loc = a_matrix.reshape(row_blocks * nb, col_blocks * nb)
    l_loc = l_panels.reshape(row_blocks * nb, 2 * nb)
    width = col_blocks * nb

    corner_piece = a_loc[:nb, :nb]
    d_half0 = jnp.where(col_id == 0, corner_piece, jnp.zeros_like(corner_piece))
    d_half1 = jnp.where(col_id == 1, corner_piece, jnp.zeros_like(corner_piece))
    for shift in range(1, col_count):
        pairs = [((i, h), (i, (h + shift) % col_count)) for i in range(2) for h in range(2)]
        got = flat_permute(corner_piece, pairs, col_count)
        d_half0 = jnp.where(col_id == shift, got, d_half0)
        d_half1 = jnp.where(col_id == (1 + shift) % col_count, got, d_half1)
    d_row = jnp.concatenate([d_half0, d_half1], 1).reshape(2 * nb, nb)

    piece = a_loc[:, :nb]
    half0 = jnp.where(col_id == 0, piece, jnp.zeros_like(piece))
    half1 = jnp.where(col_id == 1, piece, jnp.zeros_like(piece))
    for shift in range(1, col_count):
        perm = [(h, (h + shift) % col_count) for h in range(2)]
        got = lax.ppermute(piece, "col", perm)
        half0 = jnp.where(col_id == shift, got, half0)
        half1 = jnp.where(col_id == (1 + shift) % col_count, got, half1)
    z_rows = jnp.concatenate([half0, half1], 1)

    top_rows = a_matrix[0].reshape(nb * col_blocks, nb)
    payload = jnp.concatenate([top_rows, l_panels[0, 0, :, :nb], d_row], 0)
    top0, top1 = from_two_cores(payload, row_id, row_count)
    rows_end = nb * col_blocks
    b_cols = jnp.concatenate(
        [top0[:rows_end].reshape(nb, width), top1[:rows_end].reshape(nb, width)], 0
    )
    link = top1[rows_end : rows_end + nb]
    d_top = jnp.concatenate(
        [top0[rows_end + nb :].reshape(nb, 2 * nb), top1[rows_end + nb :].reshape(nb, 2 * nb)], 0
    )

    both = factor_sources(l_loc, row_id, col_id, row_count, col_count)
    l_cols = jnp.concatenate(
        [both[(k % ratio) * 2 * nb + (k // ratio) * nb :][:nb] for k in range(col_blocks)],
        0,
    )

    first_inverse = linv[0]
    second_inverse = linv[1]
    corner = -mm(second_inverse, mm(link, first_inverse))
    zero_block = jnp.zeros_like(first_inverse)
    k_top = jnp.concatenate(
        [
            jnp.concatenate([first_inverse, zero_block], 1),
            jnp.concatenate([corner, second_inverse], 1),
        ],
        0,
    )
    k_minus = k_top - jnp.eye(2 * nb, dtype=k_top.dtype)

    def u_rows(factor_rows, first_block):
        u = -mm(factor_rows, k_top)
        head = jnp.where(
            first_block == 0,
            k_minus[:nb],
            jnp.where(first_block == 1, k_minus[nb:], u[:nb]),
        )
        return jnp.concatenate([head, u[nb:]], 0)

    u_i = u_rows(l_loc, row_id)
    u_j = u_rows(l_cols, col_id)

    w_i = z_rows + mm(u_i, d_top)
    out = a_loc + mm(u_i, b_cols) + times_transposed(w_i, u_j)
    return out.reshape(a_matrix.shape)


def solution(mesh):
    in_specs = (P(None, "row", None, None, "col", None), P(None, "row", None, None), P())
    out_specs = P(None, "row", None, None, "col", None)
    return jax.shard_map(
        per_device, mesh=mesh, in_specs=in_specs, out_specs=out_specs, check_vma=False
    )
```

```python
import jax
import jax.numpy as jnp
from jax import lax
from jax.sharding import PartitionSpec as P

precise = lax.Precision.HIGHEST
AXES = ("row", "col")


def mm(left, right):
    return jnp.dot(left, right, precision=precise)


def times_transposed(left, right):
    return lax.dot_general(left, right, (((1,), (1,)), ((), ())), precision=precise)


def flat_permute(value, pairs, col_count):
    flat = [(s[0] * col_count + s[1], t[0] * col_count + t[1]) for s, t in pairs]
    return lax.ppermute(value, AXES, flat)


def cube_rounds(source_chip, bits):
    holders = [source_chip]
    rounds = []
    for bit in bits:
        step = [(h, h ^ (1 << bit)) for h in holders]
        holders = holders + [t for _, t in step]
        rounds.append(step)
    return rounds


def chip_bits(row_count):
    chips = row_count // 2
    count = chips.bit_length() - 1
    assert 1 << count == chips
    return list(range(count))


def from_two_cores(payload, row_id, row_count):
    bits = chip_bits(row_count)
    lanes = [cube_rounds(0, bits), cube_rounds(0, bits[::-1])]
    held = payload
    for step in range(len(bits)):
        perm = [
            (2 * s + core, 2 * t + core)
            for core in range(2)
            for s, t in lanes[core][step]
        ]
        got = lax.ppermute(held, "row", perm)
        held = jnp.where(row_id < 2, payload, got) if step == 0 else held + got
    mate = lax.ppermute(held, "row", [(i, i ^ 1) for i in range(row_count)])
    even = row_id % 2 == 0
    return jnp.where(even, held, mate), jnp.where(even, mate, held)


def factor_sources(l_loc, row_id, col_id, row_count, col_count):
    bits = chip_bits(row_count)
    plan = []
    for col in range(col_count):
        first, second = col, col + col_count
        k1, k2 = first // 2, second // 2
        split = ((k1 ^ k2) & -(k1 ^ k2)).bit_length() - 1
        others = [b for b in bits if b != split]
        plan.append((first % 2, k1, k2, split, cube_rounds(k1, others), cube_rounds(k2, others)))
    is_source = (row_id == col_id) | (row_id == col_id + col_count)
    held = l_loc
    for step in range(len(bits) - 1):
        pairs = []
        for col, (lane, _, _, _, rounds1, rounds2) in enumerate(plan):
            for s, t in rounds1[step] + rounds2[step]:
                pairs.append(((2 * s + lane, col), (2 * t + lane, col)))
        got = flat_permute(held, pairs, col_count)
        held = jnp.where(is_source, l_loc, got) if step == 0 else held + got
    pairs = []
    for col, (lane, _, _, split, _, _) in enumerate(plan):
        for h in range(row_count // 2):
            pairs.append(((2 * h + lane, col), (2 * (h ^ (1 << split)) + lane, col)))
    other = flat_permute(held, pairs, col_count)
    split_of = jnp.array([p[3] for p in plan], jnp.int32)[col_id]
    first_side = jnp.array([p[1] for p in plan], jnp.int32)[col_id]
    in_first = ((row_id // 2) >> split_of) % 2 == (first_side >> split_of) % 2
    both = jnp.concatenate(
        [jnp.where(in_first, held, other), jnp.where(in_first, other, held)], 0
    )
    pairs = []
    for col, (lane, _, _, _, _, _) in enumerate(plan):
        for h in range(row_count // 2):
            pairs.append(((2 * h + lane, col), (2 * h + 1 - lane, col)))
    mate = flat_permute(both, pairs, col_count)
    mine = row_id % 2 == col_id % 2
    return jnp.where(mine, both, mate)


def per_device(a_matrix, l_panels, linv):
    row_count = lax.axis_size("row")
    col_count = lax.axis_size("col")
    row_id = lax.axis_index("row")
    col_id = lax.axis_index("col")
    row_blocks = a_matrix.shape[0]
    col_blocks = a_matrix.shape[3]
    nb = a_matrix.shape[2]
    ratio = row_count // col_count
    assert ratio == 2 and row_count == ratio * col_count
    a_loc = a_matrix.reshape(row_blocks * nb, col_blocks * nb)
    l_loc = l_panels.reshape(row_blocks * nb, 2 * nb)
    width = col_blocks * nb

    top_rows = a_matrix[0].reshape(nb * col_blocks, nb)
    payload = jnp.concatenate([top_rows, l_panels[0, 0, :, :nb]], 0)
    top0, top1 = from_two_cores(payload, row_id, row_count)
    b_cols = jnp.concatenate(
        [top0[: nb * col_blocks].reshape(nb, width), top1[: nb * col_blocks].reshape(nb, width)], 0
    )
    link = top1[nb * col_blocks :]

    both = factor_sources(l_loc, row_id, col_id, row_count, col_count)
    l_cols = jnp.concatenate(
        [both[(k % ratio) * 2 * nb + (k // ratio) * nb :][:nb] for k in range(col_blocks)],
        0,
    )

    first_inverse = linv[0]
    second_inverse = linv[1]
    corner = -mm(second_inverse, mm(link, first_inverse))
    zero_block = jnp.zeros_like(first_inverse)
    k_top = jnp.concatenate(
        [
            jnp.concatenate([first_inverse, zero_block], 1),
            jnp.concatenate([corner, second_inverse], 1),
        ],
        0,
    )
    k_minus = k_top - jnp.eye(2 * nb, dtype=k_top.dtype)

    def u_rows(factor_rows, first_block):
        u = -mm(factor_rows, k_top)
        head = jnp.where(
            first_block == 0,
            k_minus[:nb],
            jnp.where(first_block == 1, k_minus[nb:], u[:nb]),
        )
        return jnp.concatenate([head, u[nb:]], 0)

    u_i = u_rows(l_loc, row_id)
    u_j = u_rows(l_cols, col_id)

    piece = a_loc[:, :nb] + mm(u_i, b_cols[:, :nb])
    half0 = jnp.where(col_id == 0, piece, jnp.zeros_like(piece))
    half1 = jnp.where(col_id == 1, piece, jnp.zeros_like(piece))
    for shift in reversed(range(1, col_count)):
        perm = [(h, (h + shift) % col_count) for h in range(2)]
        got = lax.ppermute(piece, "col", perm)
        half0 = jnp.where(col_id == shift, got, half0)
        half1 = jnp.where(col_id == (1 + shift) % col_count, got, half1)
    w_i = jnp.concatenate([half0, half1], 1)
    out = a_loc + mm(u_i, b_cols) + times_transposed(w_i, u_j)
    return out.reshape(a_matrix.shape)


def solution(mesh):
    in_specs = (P(None, "row", None, None, "col", None), P(None, "row", None, None), P())
    out_specs = P(None, "row", None, None, "col", None)
    return jax.shard_map(
        per_device, mesh=mesh, in_specs=in_specs, out_specs=out_specs, check_vma=False
    )
```

```python
import jax
import jax.numpy as jnp
from jax import lax
from jax.sharding import PartitionSpec as P

precise = lax.Precision.HIGHEST
AXES = ("row", "col")


def mm(left, right):
    return jnp.dot(left, right, precision=precise)


def times_transposed(left, right):
    return lax.dot_general(left, right, (((1,), (1,)), ((), ())), precision=precise)


def flat_permute(value, pairs, col_count):
    flat = [(s[0] * col_count + s[1], t[0] * col_count + t[1]) for s, t in pairs]
    return lax.ppermute(value, AXES, flat)


def cube_rounds(source_chip, bits):
    holders = [source_chip]
    rounds = []
    for bit in bits:
        step = [(h, h ^ (1 << bit)) for h in holders]
        holders = holders + [t for _, t in step]
        rounds.append(step)
    return rounds


def chip_bits(row_count):
    chips = row_count // 2
    count = chips.bit_length() - 1
    assert 1 << count == chips
    return list(range(count))


def from_two_cores(payload, row_id, row_count):
    bits = chip_bits(row_count)
    lanes = [cube_rounds(0, bits), cube_rounds(0, bits[::-1])]
    held = payload
    for step in range(len(bits)):
        perm = [
            (2 * s + core, 2 * t + core)
            for core in range(2)
            for s, t in lanes[core][step]
        ]
        got = lax.ppermute(held, "row", perm)
        held = jnp.where(row_id < 2, payload, got) if step == 0 else held + got
    mate = lax.ppermute(held, "row", [(i, i ^ 1) for i in range(row_count)])
    even = row_id % 2 == 0
    return jnp.where(even, held, mate), jnp.where(even, mate, held)


def factor_sources(l_loc, row_id, col_id, row_count, col_count, hold=None):
    bits = chip_bits(row_count)
    plan = []
    for col in range(col_count):
        first, second = col, col + col_count
        k1, k2 = first // 2, second // 2
        split = ((k1 ^ k2) & -(k1 ^ k2)).bit_length() - 1
        others = [b for b in bits if b != split]
        plan.append((first % 2, k1, k2, split, cube_rounds(k1, others), cube_rounds(k2, others)))
    is_source = (row_id == col_id) | (row_id == col_id + col_count)
    held = l_loc
    for step in range(len(bits) - 1):
        pairs = []
        for col, (lane, _, _, _, rounds1, rounds2) in enumerate(plan):
            for s, t in rounds1[step] + rounds2[step]:
                pairs.append(((2 * s + lane, col), (2 * t + lane, col)))
        got = flat_permute(held, pairs, col_count)
        held = jnp.where(is_source, l_loc, got) if step == 0 else held + got
    pairs = []
    for col, (lane, _, _, split, _, _) in enumerate(plan):
        for h in range(row_count // 2):
            pairs.append(((2 * h + lane, col), (2 * (h ^ (1 << split)) + lane, col)))
    other = flat_permute(held, pairs, col_count)
    split_of = jnp.array([p[3] for p in plan], jnp.int32)[col_id]
    first_side = jnp.array([p[1] for p in plan], jnp.int32)[col_id]
    in_first = ((row_id // 2) >> split_of) % 2 == (first_side >> split_of) % 2
    both = jnp.concatenate(
        [jnp.where(in_first, held, other), jnp.where(in_first, other, held)], 0
    )
    if hold is not None:
        both, hold = lax.optimization_barrier((both, hold))
    pairs = []
    for col, (lane, _, _, _, _, _) in enumerate(plan):
        for h in range(row_count // 2):
            pairs.append(((2 * h + lane, col), (2 * h + 1 - lane, col)))
    mate = flat_permute(both, pairs, col_count)
    mine = row_id % 2 == col_id % 2
    return jnp.where(mine, both, mate), hold


def per_device(a_matrix, l_panels, linv):
    row_count = lax.axis_size("row")
    col_count = lax.axis_size("col")
    row_id = lax.axis_index("row")
    col_id = lax.axis_index("col")
    row_blocks = a_matrix.shape[0]
    col_blocks = a_matrix.shape[3]
    nb = a_matrix.shape[2]
    ratio = row_count // col_count
    assert ratio == 2 and row_count == ratio * col_count
    a_loc = a_matrix.reshape(row_blocks * nb, col_blocks * nb)
    l_loc = l_panels.reshape(row_blocks * nb, 2 * nb)
    width = col_blocks * nb

    top_rows = a_matrix[0].reshape(nb * col_blocks, nb)
    payload = jnp.concatenate([top_rows, l_panels[0, 0, :, :nb]], 0)
    top0, top1 = from_two_cores(payload, row_id, row_count)
    b_cols = jnp.concatenate(
        [top0[: nb * col_blocks].reshape(nb, width), top1[: nb * col_blocks].reshape(nb, width)], 0
    )
    link = top1[nb * col_blocks :]

    first_inverse = linv[0]
    second_inverse = linv[1]
    corner = -mm(second_inverse, mm(link, first_inverse))
    zero_block = jnp.zeros_like(first_inverse)
    k_top = jnp.concatenate(
        [
            jnp.concatenate([first_inverse, zero_block], 1),
            jnp.concatenate([corner, second_inverse], 1),
        ],
        0,
    )
    k_minus = k_top - jnp.eye(2 * nb, dtype=k_top.dtype)

    def u_rows(factor_rows, first_block):
        u = -mm(factor_rows, k_top)
        head = jnp.where(
            first_block == 0,
            k_minus[:nb],
            jnp.where(first_block == 1, k_minus[nb:], u[:nb]),
        )
        return jnp.concatenate([head, u[nb:]], 0)

    u_i = u_rows(l_loc, row_id)

    piece = a_loc[:, :nb] + mm(u_i, b_cols[:, :nb])
    both, piece = factor_sources(l_loc, row_id, col_id, row_count, col_count, hold=piece)
    l_cols = jnp.concatenate(
        [both[(k % ratio) * 2 * nb + (k // ratio) * nb :][:nb] for k in range(col_blocks)],
        0,
    )

    u_j = u_rows(l_cols, col_id)
    half0 = jnp.where(col_id == 0, piece, jnp.zeros_like(piece))
    half1 = jnp.where(col_id == 1, piece, jnp.zeros_like(piece))
    for shift in reversed(range(1, col_count)):
        perm = [(h, (h + shift) % col_count) for h in range(2)]
        got = lax.ppermute(piece, "col", perm)
        half0 = jnp.where(col_id == shift, got, half0)
        half1 = jnp.where(col_id == (1 + shift) % col_count, got, half1)
    w_i = jnp.concatenate([half0, half1], 1)
    out = a_loc + mm(u_i, b_cols) + times_transposed(w_i, u_j)
    return out.reshape(a_matrix.shape)


def solution(mesh):
    in_specs = (P(None, "row", None, None, "col", None), P(None, "row", None, None), P())
    out_specs = P(None, "row", None, None, "col", None)
    return jax.shard_map(
        per_device, mesh=mesh, in_specs=in_specs, out_specs=out_specs, check_vma=False
    )
```

```python
import jax
import jax.numpy as jnp
from jax import lax
from jax.sharding import PartitionSpec as P

precise = lax.Precision.HIGHEST
AXES = ("row", "col")


def mm(left, right):
    return jnp.dot(left, right, precision=precise)


def times_transposed(left, right):
    return lax.dot_general(left, right, (((1,), (1,)), ((), ())), precision=precise)


def flat_permute(value, pairs, col_count):
    flat = [(s[0] * col_count + s[1], t[0] * col_count + t[1]) for s, t in pairs]
    return lax.ppermute(value, AXES, flat)


def cube_rounds(source_chip, bits):
    holders = [source_chip]
    rounds = []
    for bit in bits:
        step = [(h, h ^ (1 << bit)) for h in holders]
        holders = holders + [t for _, t in step]
        rounds.append(step)
    return rounds


def chip_bits(row_count):
    chips = row_count // 2
    count = chips.bit_length() - 1
    assert 1 << count == chips
    return list(range(count))


def from_two_cores(payload, row_id, row_count):
    bits = chip_bits(row_count)
    lanes = [cube_rounds(0, bits), cube_rounds(0, bits[::-1])]
    held = payload
    for step in range(len(bits)):
        perm = [
            (2 * s + core, 2 * t + core)
            for core in range(2)
            for s, t in lanes[core][step]
        ]
        got = lax.ppermute(held, "row", perm)
        held = jnp.where(row_id < 2, payload, got) if step == 0 else held + got
    return held


def factor_sources(l_loc, row_id, col_id, row_count, col_count):
    bits = chip_bits(row_count)
    plan = []
    for col in range(col_count):
        first, second = col, col + col_count
        k1, k2 = first // 2, second // 2
        split = ((k1 ^ k2) & -(k1 ^ k2)).bit_length() - 1
        others = [b for b in bits if b != split]
        plan.append((first % 2, k1, k2, split, cube_rounds(k1, others), cube_rounds(k2, others)))
    is_source = (row_id == col_id) | (row_id == col_id + col_count)
    held = l_loc
    for step in range(len(bits) - 1):
        pairs = []
        for col, (lane, _, _, _, rounds1, rounds2) in enumerate(plan):
            for s, t in rounds1[step] + rounds2[step]:
                pairs.append(((2 * s + lane, col), (2 * t + lane, col)))
        got = flat_permute(held, pairs, col_count)
        held = jnp.where(is_source, l_loc, got) if step == 0 else held + got
    pairs = []
    for col, (lane, _, _, split, _, _) in enumerate(plan):
        for h in range(row_count // 2):
            pairs.append(((2 * h + lane, col), (2 * (h ^ (1 << split)) + lane, col)))
    other = flat_permute(held, pairs, col_count)
    split_of = jnp.array([p[3] for p in plan], jnp.int32)[col_id]
    first_side = jnp.array([p[1] for p in plan], jnp.int32)[col_id]
    in_first = ((row_id // 2) >> split_of) % 2 == (first_side >> split_of) % 2
    both = jnp.concatenate(
        [jnp.where(in_first, held, other), jnp.where(in_first, other, held)], 0
    )
    return both


def per_device(a_matrix, l_panels, linv):
    row_count = lax.axis_size("row")
    col_count = lax.axis_size("col")
    row_id = lax.axis_index("row")
    col_id = lax.axis_index("col")
    row_blocks = a_matrix.shape[0]
    col_blocks = a_matrix.shape[3]
    nb = a_matrix.shape[2]
    ratio = row_count // col_count
    assert ratio == 2 and row_count == ratio * col_count
    a_loc = a_matrix.reshape(row_blocks * nb, col_blocks * nb)
    l_loc = l_panels.reshape(row_blocks * nb, 2 * nb)
    width = col_blocks * nb

    top_rows = a_matrix[0].reshape(nb * col_blocks, nb)
    payload = jnp.concatenate([top_rows, l_panels[0, 0, :, :nb]], 0)
    held = from_two_cores(payload, row_id, row_count)
    both = factor_sources(l_loc, row_id, col_id, row_count, col_count)
    rows = held.shape[0]
    merged = jnp.concatenate([held, both.reshape(-1, nb)], 0)
    mate = lax.ppermute(merged, "row", [(i, i ^ 1) for i in range(row_count)])
    even = row_id % 2 == 0
    top0 = jnp.where(even, held, mate[:rows])
    top1 = jnp.where(even, mate[:rows], held)
    both = jnp.where(row_id % 2 == col_id % 2, both, mate[rows:].reshape(both.shape))
    b_cols = jnp.concatenate(
        [top0[: nb * col_blocks].reshape(nb, width), top1[: nb * col_blocks].reshape(nb, width)], 0
    )
    link = top1[nb * col_blocks :]

    l_cols = jnp.concatenate(
        [both[(k % ratio) * 2 * nb + (k // ratio) * nb :][:nb] for k in range(col_blocks)],
        0,
    )

    first_inverse = linv[0]
    second_inverse = linv[1]
    corner = -mm(second_inverse, mm(link, first_inverse))
    zero_block = jnp.zeros_like(first_inverse)
    k_top = jnp.concatenate(
        [
            jnp.concatenate([first_inverse, zero_block], 1),
            jnp.concatenate([corner, second_inverse], 1),
        ],
        0,
    )
    k_minus = k_top - jnp.eye(2 * nb, dtype=k_top.dtype)

    def u_rows(factor_rows, first_block):
        u = -mm(factor_rows, k_top)
        head = jnp.where(
            first_block == 0,
            k_minus[:nb],
            jnp.where(first_block == 1, k_minus[nb:], u[:nb]),
        )
        return jnp.concatenate([head, u[nb:]], 0)

    u_i = u_rows(l_loc, row_id)
    u_j = u_rows(l_cols, col_id)

    piece = a_loc[:, :nb] + mm(u_i, b_cols[:, :nb])
    half0 = jnp.where(col_id == 0, piece, jnp.zeros_like(piece))
    half1 = jnp.where(col_id == 1, piece, jnp.zeros_like(piece))
    for shift in reversed(range(1, col_count)):
        perm = [(h, (h + shift) % col_count) for h in range(2)]
        got = lax.ppermute(piece, "col", perm)
        half0 = jnp.where(col_id == shift, got, half0)
        half1 = jnp.where(col_id == (1 + shift) % col_count, got, half1)
    w_i = jnp.concatenate([half0, half1], 1)
    out = a_loc + mm(u_i, b_cols) + times_transposed(w_i, u_j)
    return out.reshape(a_matrix.shape)


def solution(mesh):
    in_specs = (P(None, "row", None, None, "col", None), P(None, "row", None, None), P())
    out_specs = P(None, "row", None, None, "col", None)
    return jax.shard_map(
        per_device, mesh=mesh, in_specs=in_specs, out_specs=out_specs, check_vma=False
    )
```

```python
import jax
import jax.numpy as jnp
from jax import lax
from jax.sharding import PartitionSpec as P

precise = lax.Precision.HIGHEST
AXES = ("row", "col")


def mm(left, right):
    return jnp.dot(left, right, precision=precise)


def times_transposed(left, right):
    return lax.dot_general(left, right, (((1,), (1,)), ((), ())), precision=precise)


def flat_permute(value, pairs, col_count):
    flat = [(s[0] * col_count + s[1], t[0] * col_count + t[1]) for s, t in pairs]
    return lax.ppermute(value, AXES, flat)


def cube_rounds(source_chip, bits):
    holders = [source_chip]
    rounds = []
    for bit in bits:
        step = [(h, h ^ (1 << bit)) for h in holders]
        holders = holders + [t for _, t in step]
        rounds.append(step)
    return rounds


def chip_bits(row_count):
    chips = row_count // 2
    count = chips.bit_length() - 1
    assert 1 << count == chips
    return list(range(count))


def from_two_cores(payload, row_id, row_count):
    bits = chip_bits(row_count)
    lanes = [cube_rounds(0, bits), cube_rounds(0, bits[::-1])]
    held = payload
    for step in range(len(bits)):
        perm = [
            (2 * s + core, 2 * t + core)
            for core in range(2)
            for s, t in lanes[core][step]
        ]
        got = lax.ppermute(held, "row", perm)
        held = jnp.where(row_id < 2, payload, got) if step == 0 else held + got
    mate = lax.ppermute(held, "row", [(i, i ^ 1) for i in range(row_count)])
    even = row_id % 2 == 0
    return jnp.where(even, held, mate), jnp.where(even, mate, held)


def factor_sources(l_loc, row_id, col_id, row_count, col_count):
    bits = chip_bits(row_count)
    plan = []
    for col in range(col_count):
        first, second = col, col + col_count
        k1, k2 = first // 2, second // 2
        split = ((k1 ^ k2) & -(k1 ^ k2)).bit_length() - 1
        others = [b for b in bits if b != split]
        plan.append((first % 2, k1, k2, split, cube_rounds(k1, others), cube_rounds(k2, others)))
    is_source = (row_id == col_id) | (row_id == col_id + col_count)
    held = l_loc
    for step in range(len(bits) - 1):
        pairs = []
        for col, (lane, _, _, _, rounds1, rounds2) in enumerate(plan):
            for s, t in rounds1[step] + rounds2[step]:
                pairs.append(((2 * s + lane, col), (2 * t + lane, col)))
        got = flat_permute(held, pairs, col_count)
        held = jnp.where(is_source, l_loc, got) if step == 0 else held + got
    pairs = []
    for col, (lane, _, _, split, _, _) in enumerate(plan):
        for h in range(row_count // 2):
            pairs.append(((2 * h + lane, col), (2 * (h ^ (1 << split)) + lane, col)))
    other = flat_permute(held, pairs, col_count)
    split_of = jnp.array([p[3] for p in plan], jnp.int32)[col_id]
    first_side = jnp.array([p[1] for p in plan], jnp.int32)[col_id]
    in_first = ((row_id // 2) >> split_of) % 2 == (first_side >> split_of) % 2
    both = jnp.concatenate(
        [jnp.where(in_first, held, other), jnp.where(in_first, other, held)], 0
    )
    pairs = []
    for col, (lane, _, _, _, _, _) in enumerate(plan):
        for h in range(row_count // 2):
            pairs.append(((2 * h + lane, col), (2 * h + 1 - lane, col)))
    mate = flat_permute(both, pairs, col_count)
    mine = row_id % 2 == col_id % 2
    return jnp.where(mine, both, mate)


def per_device(a_matrix, l_panels, linv):
    row_count = lax.axis_size("row")
    col_count = lax.axis_size("col")
    row_id = lax.axis_index("row")
    col_id = lax.axis_index("col")
    row_blocks = a_matrix.shape[0]
    col_blocks = a_matrix.shape[3]
    nb = a_matrix.shape[2]
    ratio = row_count // col_count
    assert ratio == 2 and row_count == ratio * col_count
    a_loc = a_matrix.reshape(row_blocks * nb, col_blocks * nb)
    l_loc = l_panels.reshape(row_blocks * nb, 2 * nb)
    width = col_blocks * nb

    top_rows = a_matrix[0].reshape(nb * col_blocks, nb)
    payload = jnp.concatenate([top_rows, l_panels[0, 0, :, :nb]], 0)
    top0, top1 = from_two_cores(payload, row_id, row_count)
    b_cols = jnp.concatenate(
        [top0[: nb * col_blocks].reshape(nb, width), top1[: nb * col_blocks].reshape(nb, width)], 0
    )
    link = top1[nb * col_blocks :]

    both = factor_sources(l_loc, row_id, col_id, row_count, col_count)
    l_cols = jnp.concatenate(
        [both[(k % ratio) * 2 * nb + (k // ratio) * nb :][:nb] for k in range(col_blocks)],
        0,
    )

    first_inverse = linv[0]
    second_inverse = linv[1]
    corner = -mm(second_inverse, mm(link, first_inverse))
    zero_block = jnp.zeros_like(first_inverse)
    k_top = jnp.concatenate(
        [
            jnp.concatenate([first_inverse, zero_block], 1),
            jnp.concatenate([corner, second_inverse], 1),
        ],
        0,
    )
    k_minus = k_top - jnp.eye(2 * nb, dtype=k_top.dtype)

    def u_rows(factor_rows, first_block):
        u = -mm(factor_rows, k_top)
        head = jnp.where(
            first_block == 0,
            k_minus[:nb],
            jnp.where(first_block == 1, k_minus[nb:], u[:nb]),
        )
        return jnp.concatenate([head, u[nb:]], 0)

    u_i = u_rows(l_loc, row_id)
    u_j = u_rows(l_cols, col_id)

    piece = a_loc[:, :nb] + mm(u_i, b_cols[:, :nb])
    spread = jnp.broadcast_to(piece[None], (col_count,) + piece.shape)
    gathered = lax.all_to_all(spread, "col", 0, 0)
    w_i = jnp.concatenate([gathered[0], gathered[1]], 1)
    out = a_loc + mm(u_i, b_cols) + times_transposed(w_i, u_j)
    return out.reshape(a_matrix.shape)


def solution(mesh):
    in_specs = (P(None, "row", None, None, "col", None), P(None, "row", None, None), P())
    out_specs = P(None, "row", None, None, "col", None)
    return jax.shard_map(
        per_device, mesh=mesh, in_specs=in_specs, out_specs=out_specs, check_vma=False
    )
```

```python
import jax
import jax.numpy as jnp
from jax import lax
from jax.sharding import PartitionSpec as P

precise = lax.Precision.HIGHEST
AXES = ("row", "col")


def mm(left, right):
    return jnp.dot(left, right, precision=precise)


def times_transposed(left, right):
    return lax.dot_general(left, right, (((1,), (1,)), ((), ())), precision=precise)


def flat_permute(value, pairs, col_count):
    flat = [(s[0] * col_count + s[1], t[0] * col_count + t[1]) for s, t in pairs]
    return lax.ppermute(value, AXES, flat)


def cube_rounds(source_chip, bits):
    holders = [source_chip]
    rounds = []
    for bit in bits:
        step = [(h, h ^ (1 << bit)) for h in holders]
        holders = holders + [t for _, t in step]
        rounds.append(step)
    return rounds


def chip_bits(row_count):
    chips = row_count // 2
    count = chips.bit_length() - 1
    assert 1 << count == chips
    return list(range(count))


def from_two_cores(payload, row_id, row_count):
    bits = chip_bits(row_count)
    lanes = [cube_rounds(0, bits), cube_rounds(0, bits[::-1])]
    held = payload
    for step in range(len(bits)):
        perm = [
            (2 * s + core, 2 * t + core)
            for core in range(2)
            for s, t in lanes[core][step]
        ]
        got = lax.ppermute(held, "row", perm)
        held = jnp.where(row_id < 2, payload, got) if step == 0 else held + got
    mate = lax.ppermute(held, "row", [(i, i ^ 1) for i in range(row_count)])
    even = row_id % 2 == 0
    return jnp.where(even, held, mate), jnp.where(even, mate, held)


def factor_sources(l_loc, row_id, col_id, row_count, col_count):
    bits = chip_bits(row_count)
    plan = []
    for col in range(col_count):
        first, second = col, col + col_count
        k1, k2 = first // 2, second // 2
        split = ((k1 ^ k2) & -(k1 ^ k2)).bit_length() - 1
        others = [b for b in bits if b != split]
        plan.append((first % 2, k1, k2, split, cube_rounds(k1, others), cube_rounds(k2, others)))
    is_source = (row_id == col_id) | (row_id == col_id + col_count)
    held = l_loc
    for step in range(len(bits) - 1):
        pairs = []
        for col, (lane, _, _, _, rounds1, rounds2) in enumerate(plan):
            for s, t in rounds1[step] + rounds2[step]:
                pairs.append(((2 * s + lane, col), (2 * t + lane, col)))
        got = flat_permute(held, pairs, col_count)
        held = jnp.where(is_source, l_loc, got) if step == 0 else held + got
    pairs = []
    for col, (lane, _, _, split, _, _) in enumerate(plan):
        for h in range(row_count // 2):
            pairs.append(((2 * h + lane, col), (2 * (h ^ (1 << split)) + lane, col)))
    other = flat_permute(held, pairs, col_count)
    split_of = jnp.array([p[3] for p in plan], jnp.int32)[col_id]
    first_side = jnp.array([p[1] for p in plan], jnp.int32)[col_id]
    in_first = ((row_id // 2) >> split_of) % 2 == (first_side >> split_of) % 2
    both = jnp.concatenate(
        [jnp.where(in_first, held, other), jnp.where(in_first, other, held)], 0
    )
    pairs = []
    for col, (lane, _, _, _, _, _) in enumerate(plan):
        for h in range(row_count // 2):
            pairs.append(((2 * h + lane, col), (2 * h + 1 - lane, col)))
    mate = flat_permute(both, pairs, col_count)
    mine = row_id % 2 == col_id % 2
    return jnp.where(mine, both, mate)


def per_device(a_matrix, l_panels, linv):
    row_count = lax.axis_size("row")
    col_count = lax.axis_size("col")
    row_id = lax.axis_index("row")
    col_id = lax.axis_index("col")
    row_blocks = a_matrix.shape[0]
    col_blocks = a_matrix.shape[3]
    nb = a_matrix.shape[2]
    ratio = row_count // col_count
    assert ratio == 2 and row_count == ratio * col_count
    a_loc = a_matrix.reshape(row_blocks * nb, col_blocks * nb)
    l_loc = l_panels.reshape(row_blocks * nb, 2 * nb)
    width = col_blocks * nb

    top_rows = a_matrix[0].reshape(nb * col_blocks, nb)
    payload = jnp.concatenate([top_rows, l_panels[0, 0, :, :nb]], 0)
    top0, top1 = from_two_cores(payload, row_id, row_count)
    b_cols = jnp.concatenate(
        [top0[: nb * col_blocks].reshape(nb, width), top1[: nb * col_blocks].reshape(nb, width)], 0
    )
    link = top1[nb * col_blocks :]

    both = factor_sources(l_loc, row_id, col_id, row_count, col_count)
    l_cols = jnp.concatenate(
        [both[(k % ratio) * 2 * nb + (k // ratio) * nb :][:nb] for k in range(col_blocks)],
        0,
    )

    first_inverse = linv[0]
    second_inverse = linv[1]
    corner = -mm(second_inverse, mm(link, first_inverse))
    zero_block = jnp.zeros_like(first_inverse)
    k_top = jnp.concatenate(
        [
            jnp.concatenate([first_inverse, zero_block], 1),
            jnp.concatenate([corner, second_inverse], 1),
        ],
        0,
    )
    k_minus = k_top - jnp.eye(2 * nb, dtype=k_top.dtype)

    def u_rows(factor_rows, first_block):
        u = -mm(factor_rows, k_top)
        head = jnp.where(
            first_block == 0,
            k_minus[:nb],
            jnp.where(first_block == 1, k_minus[nb:], u[:nb]),
        )
        return jnp.concatenate([head, u[nb:]], 0)

    u_i = u_rows(l_loc, row_id)
    u_j = u_rows(l_cols, col_id)

    piece = a_loc[:, :nb] + mm(u_i, b_cols[:, :nb])
    half0 = jnp.where(col_id == 0, piece, jnp.zeros_like(piece))
    half1 = jnp.where(col_id == 1, piece, jnp.zeros_like(piece))
    for shift in [1] + list(reversed(range(2, col_count))):
        perm = [(h, (h + shift) % col_count) for h in range(2)]
        got = lax.ppermute(piece, "col", perm)
        half0 = jnp.where(col_id == shift, got, half0)
        half1 = jnp.where(col_id == (1 + shift) % col_count, got, half1)
    w_i = jnp.concatenate([half0, half1], 1)
    out = a_loc + mm(u_i, b_cols) + times_transposed(w_i, u_j)
    return out.reshape(a_matrix.shape)


def solution(mesh):
    in_specs = (P(None, "row", None, None, "col", None), P(None, "row", None, None), P())
    out_specs = P(None, "row", None, None, "col", None)
    return jax.shard_map(
        per_device, mesh=mesh, in_specs=in_specs, out_specs=out_specs, check_vma=False
    )
```

```python
import jax
import jax.numpy as jnp
from jax import lax
from jax.sharding import PartitionSpec as P

precise = lax.Precision.HIGHEST
AXES = ("row", "col")


def mm(left, right):
    return jnp.dot(left, right, precision=precise)


def times_transposed(left, right):
    return lax.dot_general(left, right, (((1,), (1,)), ((), ())), precision=precise)


def flat_permute(value, pairs, col_count):
    flat = [(s[0] * col_count + s[1], t[0] * col_count + t[1]) for s, t in pairs]
    return lax.ppermute(value, AXES, flat)


def cube_rounds(source_chip, bits):
    holders = [source_chip]
    rounds = []
    for bit in bits:
        step = [(h, h ^ (1 << bit)) for h in holders]
        holders = holders + [t for _, t in step]
        rounds.append(step)
    return rounds


def chip_bits(row_count):
    chips = row_count // 2
    count = chips.bit_length() - 1
    assert 1 << count == chips
    return list(range(count))


def from_two_cores(payload, row_id, row_count):
    bits = chip_bits(row_count)
    lanes = [cube_rounds(0, bits), cube_rounds(0, bits[::-1])]
    held = payload
    for step in range(len(bits)):
        perm = [
            (2 * s + core, 2 * t + core)
            for core in range(2)
            for s, t in lanes[core][step]
        ]
        got = lax.ppermute(held, "row", perm)
        held = jnp.where(row_id < 2, payload, got) if step == 0 else held + got
    mate = lax.ppermute(held, "row", [(i, i ^ 1) for i in range(row_count)])
    even = row_id % 2 == 0
    return jnp.where(even, held, mate), jnp.where(even, mate, held)


def factor_sources(l_loc, row_id, col_id, row_count, col_count):
    bits = chip_bits(row_count)
    plan = []
    for col in range(col_count):
        first, second = col, col + col_count
        k1, k2 = first // 2, second // 2
        split = ((k1 ^ k2) & -(k1 ^ k2)).bit_length() - 1
        others = [b for b in bits if b != split]
        plan.append((first % 2, k1, k2, split, cube_rounds(k1, others), cube_rounds(k2, others)))
    is_source = (row_id == col_id) | (row_id == col_id + col_count)
    held = l_loc
    for step in range(len(bits) - 1):
        pairs = []
        for col, (lane, _, _, _, rounds1, rounds2) in enumerate(plan):
            for s, t in rounds1[step] + rounds2[step]:
                pairs.append(((2 * s + lane, col), (2 * t + lane, col)))
        got = flat_permute(held, pairs, col_count)
        held = jnp.where(is_source, l_loc, got) if step == 0 else held + got
    pairs = []
    for col, (lane, _, _, split, _, _) in enumerate(plan):
        for h in range(row_count // 2):
            pairs.append(((2 * h + lane, col), (2 * (h ^ (1 << split)) + lane, col)))
    other = flat_permute(held, pairs, col_count)
    split_of = jnp.array([p[3] for p in plan], jnp.int32)[col_id]
    first_side = jnp.array([p[1] for p in plan], jnp.int32)[col_id]
    in_first = ((row_id // 2) >> split_of) % 2 == (first_side >> split_of) % 2
    both = jnp.concatenate(
        [jnp.where(in_first, held, other), jnp.where(in_first, other, held)], 0
    )
    pairs = []
    for col, (lane, _, _, _, _, _) in enumerate(plan):
        for h in range(row_count // 2):
            pairs.append(((2 * h + lane, col), (2 * h + 1 - lane, col)))
    mate = flat_permute(both, pairs, col_count)
    mine = row_id % 2 == col_id % 2
    return jnp.where(mine, both, mate)


def per_device(a_matrix, l_panels, linv):
    row_count = lax.axis_size("row")
    col_count = lax.axis_size("col")
    row_id = lax.axis_index("row")
    col_id = lax.axis_index("col")
    row_blocks = a_matrix.shape[0]
    col_blocks = a_matrix.shape[3]
    nb = a_matrix.shape[2]
    ratio = row_count // col_count
    assert ratio == 2 and row_count == ratio * col_count
    a_loc = a_matrix.reshape(row_blocks * nb, col_blocks * nb)
    l_loc = l_panels.reshape(row_blocks * nb, 2 * nb)
    width = col_blocks * nb

    top_rows = a_matrix[0].reshape(nb * col_blocks, nb)
    payload = jnp.concatenate([top_rows, l_panels[0, 0, :, :nb]], 0)
    top0, top1 = from_two_cores(payload, row_id, row_count)
    b_cols = jnp.concatenate(
        [top0[: nb * col_blocks].reshape(nb, width), top1[: nb * col_blocks].reshape(nb, width)], 0
    )
    link = top1[nb * col_blocks :]

    both = factor_sources(l_loc, row_id, col_id, row_count, col_count)
    first_inverse = linv[0]
    second_inverse = linv[1]
    corner = -mm(second_inverse, mm(link, first_inverse))
    zero_block = jnp.zeros_like(first_inverse)
    k_top = jnp.concatenate(
        [
            jnp.concatenate([first_inverse, zero_block], 1),
            jnp.concatenate([corner, second_inverse], 1),
        ],
        0,
    )
    k_minus = k_top - jnp.eye(2 * nb, dtype=k_top.dtype)

    def u_rows(factor_rows, first_block):
        u = -mm(factor_rows, k_top)
        head = jnp.where(
            first_block == 0,
            k_minus[:nb],
            jnp.where(first_block == 1, k_minus[nb:], u[:nb]),
        )
        return jnp.concatenate([head, u[nb:]], 0)

    u_i = u_rows(l_loc, row_id)

    piece = a_loc[:, :nb] + mm(u_i, b_cols[:, :nb])
    both, piece = lax.optimization_barrier((both, piece))
    l_cols = jnp.concatenate(
        [both[(k % ratio) * 2 * nb + (k // ratio) * nb :][:nb] for k in range(col_blocks)],
        0,
    )

    u_j = u_rows(l_cols, col_id)
    half0 = jnp.where(col_id == 0, piece, jnp.zeros_like(piece))
    half1 = jnp.where(col_id == 1, piece, jnp.zeros_like(piece))
    for shift in [1] + list(reversed(range(2, col_count))):
        perm = [(h, (h + shift) % col_count) for h in range(2)]
        got = lax.ppermute(piece, "col", perm)
        half0 = jnp.where(col_id == shift, got, half0)
        half1 = jnp.where(col_id == (1 + shift) % col_count, got, half1)
    w_i = jnp.concatenate([half0, half1], 1)
    out = a_loc + mm(u_i, b_cols) + times_transposed(w_i, u_j)
    return out.reshape(a_matrix.shape)


def solution(mesh):
    in_specs = (P(None, "row", None, None, "col", None), P(None, "row", None, None), P())
    out_specs = P(None, "row", None, None, "col", None)
    return jax.shard_map(
        per_device, mesh=mesh, in_specs=in_specs, out_specs=out_specs, check_vma=False
    )
```

```python
import jax
import jax.numpy as jnp
from jax import lax
from jax.sharding import PartitionSpec as P

precise = lax.Precision.HIGHEST
AXES = ("row", "col")


def mm(left, right):
    return jnp.dot(left, right, precision=precise)


def times_transposed(left, right):
    return lax.dot_general(left, right, (((1,), (1,)), ((), ())), precision=precise)


def flat_permute(value, pairs, col_count):
    flat = [(s[0] * col_count + s[1], t[0] * col_count + t[1]) for s, t in pairs]
    return lax.ppermute(value, AXES, flat)


def cube_rounds(source_chip, bits):
    holders = [source_chip]
    rounds = []
    for bit in bits:
        step = [(h, h ^ (1 << bit)) for h in holders]
        holders = holders + [t for _, t in step]
        rounds.append(step)
    return rounds


def chip_bits(row_count):
    chips = row_count // 2
    count = chips.bit_length() - 1
    assert 1 << count == chips
    return list(range(count))


def from_two_cores(payload, row_id, row_count):
    bits = chip_bits(row_count)
    lanes = [cube_rounds(0, bits), cube_rounds(0, bits[::-1])]
    held = payload
    for step in range(len(bits)):
        perm = [
            (2 * s + core, 2 * t + core)
            for core in range(2)
            for s, t in lanes[core][step]
        ]
        got = lax.ppermute(held, "row", perm)
        held = jnp.where(row_id < 2, payload, got) if step == 0 else held + got
    mate = lax.ppermute(held, "row", [(i, i ^ 1) for i in range(row_count)])
    even = row_id % 2 == 0
    return jnp.where(even, held, mate), jnp.where(even, mate, held)


def factor_sources(l_loc, row_id, col_id, row_count, col_count):
    bits = chip_bits(row_count)
    plan = []
    for col in range(col_count):
        first, second = col, col + col_count
        k1, k2 = first // 2, second // 2
        split = ((k1 ^ k2) & -(k1 ^ k2)).bit_length() - 1
        others = [b for b in bits if b != split]
        plan.append((first % 2, k1, k2, split, cube_rounds(k1, others), cube_rounds(k2, others)))
    is_source = (row_id == col_id) | (row_id == col_id + col_count)
    held = l_loc
    for step in range(len(bits) - 1):
        pairs = []
        for col, (lane, _, _, _, rounds1, rounds2) in enumerate(plan):
            for s, t in rounds1[step] + rounds2[step]:
                pairs.append(((2 * s + lane, col), (2 * t + lane, col)))
        got = flat_permute(held, pairs, col_count)
        held = jnp.where(is_source, l_loc, got) if step == 0 else held + got
    pairs = []
    for col, (lane, _, _, split, _, _) in enumerate(plan):
        for h in range(row_count // 2):
            pairs.append(((2 * h + lane, col), (2 * (h ^ (1 << split)) + lane, col)))
    other = flat_permute(held, pairs, col_count)
    split_of = jnp.array([p[3] for p in plan], jnp.int32)[col_id]
    first_side = jnp.array([p[1] for p in plan], jnp.int32)[col_id]
    in_first = ((row_id // 2) >> split_of) % 2 == (first_side >> split_of) % 2
    both = jnp.concatenate(
        [jnp.where(in_first, held, other), jnp.where(in_first, other, held)], 0
    )
    pairs = []
    for col, (lane, _, _, _, _, _) in enumerate(plan):
        for h in range(row_count // 2):
            pairs.append(((2 * h + lane, col), (2 * h + 1 - lane, col)))
    mate = flat_permute(both, pairs, col_count)
    mine = row_id % 2 == col_id % 2
    return jnp.where(mine, both, mate)


def per_device(a_matrix, l_panels, linv):
    row_count = lax.axis_size("row")
    col_count = lax.axis_size("col")
    row_id = lax.axis_index("row")
    col_id = lax.axis_index("col")
    row_blocks = a_matrix.shape[0]
    col_blocks = a_matrix.shape[3]
    nb = a_matrix.shape[2]
    ratio = row_count // col_count
    assert ratio == 2 and row_count == ratio * col_count
    a_loc = a_matrix.reshape(row_blocks * nb, col_blocks * nb)
    l_loc = l_panels.reshape(row_blocks * nb, 2 * nb)
    width = col_blocks * nb

    top_rows = a_matrix[0].reshape(nb * col_blocks, nb)
    payload = jnp.concatenate([top_rows, l_panels[0, 0, :, :nb]], 0)
    top0, top1 = from_two_cores(payload, row_id, row_count)
    b_cols = jnp.concatenate(
        [top0[: nb * col_blocks].reshape(nb, width), top1[: nb * col_blocks].reshape(nb, width)], 0
    )
    link = top1[nb * col_blocks :]

    both = factor_sources(l_loc, row_id, col_id, row_count, col_count)
    l_cols = jnp.concatenate(
        [both[(k % ratio) * 2 * nb + (k // ratio) * nb :][:nb] for k in range(col_blocks)],
        0,
    )

    first_inverse = linv[0]
    second_inverse = linv[1]
    corner = -mm(second_inverse, mm(link, first_inverse))
    zero_block = jnp.zeros_like(first_inverse)
    k_top = jnp.concatenate(
        [
            jnp.concatenate([first_inverse, zero_block], 1),
            jnp.concatenate([corner, second_inverse], 1),
        ],
        0,
    )
    k_minus = k_top - jnp.eye(2 * nb, dtype=k_top.dtype)

    def u_rows(factor_rows, first_block):
        u = -mm(factor_rows, k_top)
        head = jnp.where(
            first_block == 0,
            k_minus[:nb],
            jnp.where(first_block == 1, k_minus[nb:], u[:nb]),
        )
        return jnp.concatenate([head, u[nb:]], 0)

    u_i = u_rows(l_loc, row_id)
    u_j = u_rows(l_cols, col_id)

    piece = a_loc[:, :nb] + mm(u_i, b_cols[:, :nb])
    half0 = jnp.where(col_id == 0, piece, jnp.zeros_like(piece))
    half1 = jnp.where(col_id == 1, piece, jnp.zeros_like(piece))
    for shift in list(reversed(range(3, col_count))) + [1, 2][: col_count - 1]:
        perm = [(h, (h + shift) % col_count) for h in range(2)]
        got = lax.ppermute(piece, "col", perm)
        half0 = jnp.where(col_id == shift, got, half0)
        half1 = jnp.where(col_id == (1 + shift) % col_count, got, half1)
    w_i = jnp.concatenate([half0, half1], 1)
    out = a_loc + mm(u_i, b_cols) + times_transposed(w_i, u_j)
    return out.reshape(a_matrix.shape)


def solution(mesh):
    in_specs = (P(None, "row", None, None, "col", None), P(None, "row", None, None), P())
    out_specs = P(None, "row", None, None, "col", None)
    return jax.shard_map(
        per_device, mesh=mesh, in_specs=in_specs, out_specs=out_specs, check_vma=False
    )
```

```python
import jax
import jax.numpy as jnp
from jax import lax
from jax.sharding import PartitionSpec as P

precise = lax.Precision.HIGHEST
AXES = ("row", "col")


def mm(left, right):
    return jnp.dot(left, right, precision=precise)


def times_transposed(left, right):
    return lax.dot_general(left, right, (((1,), (1,)), ((), ())), precision=precise)


def flat_permute(value, pairs, col_count):
    flat = [(s[0] * col_count + s[1], t[0] * col_count + t[1]) for s, t in pairs]
    return lax.ppermute(value, AXES, flat)


def cube_rounds(source_chip, bits):
    holders = [source_chip]
    rounds = []
    for bit in bits:
        step = [(h, h ^ (1 << bit)) for h in holders]
        holders = holders + [t for _, t in step]
        rounds.append(step)
    return rounds


def chip_bits(row_count):
    chips = row_count // 2
    count = chips.bit_length() - 1
    assert 1 << count == chips
    return list(range(count))


def from_two_cores(payload, row_id, row_count):
    bits = chip_bits(row_count)
    lanes = [cube_rounds(0, bits[::-1]), cube_rounds(0, bits)]
    held = payload
    for step in range(len(bits)):
        perm = [
            (2 * s + core, 2 * t + core)
            for core in range(2)
            for s, t in lanes[core][step]
        ]
        got = lax.ppermute(held, "row", perm)
        held = jnp.where(row_id < 2, payload, got) if step == 0 else held + got
    mate = lax.ppermute(held, "row", [(i, i ^ 1) for i in range(row_count)])
    even = row_id % 2 == 0
    return jnp.where(even, held, mate), jnp.where(even, mate, held)


def factor_sources(l_loc, row_id, col_id, row_count, col_count):
    bits = chip_bits(row_count)
    plan = []
    for col in range(col_count):
        first, second = col, col + col_count
        k1, k2 = first // 2, second // 2
        split = ((k1 ^ k2) & -(k1 ^ k2)).bit_length() - 1
        others = [b for b in bits if b != split]
        plan.append((first % 2, k1, k2, split, cube_rounds(k1, others), cube_rounds(k2, others)))
    is_source = (row_id == col_id) | (row_id == col_id + col_count)
    held = l_loc
    for step in range(len(bits) - 1):
        pairs = []
        for col, (lane, _, _, _, rounds1, rounds2) in enumerate(plan):
            for s, t in rounds1[step] + rounds2[step]:
                pairs.append(((2 * s + lane, col), (2 * t + lane, col)))
        got = flat_permute(held, pairs, col_count)
        held = jnp.where(is_source, l_loc, got) if step == 0 else held + got
    pairs = []
    for col, (lane, _, _, split, _, _) in enumerate(plan):
        for h in range(row_count // 2):
            pairs.append(((2 * h + lane, col), (2 * (h ^ (1 << split)) + lane, col)))
    other = flat_permute(held, pairs, col_count)
    split_of = jnp.array([p[3] for p in plan], jnp.int32)[col_id]
    first_side = jnp.array([p[1] for p in plan], jnp.int32)[col_id]
    in_first = ((row_id // 2) >> split_of) % 2 == (first_side >> split_of) % 2
    both = jnp.concatenate(
        [jnp.where(in_first, held, other), jnp.where(in_first, other, held)], 0
    )
    pairs = []
    for col, (lane, _, _, _, _, _) in enumerate(plan):
        for h in range(row_count // 2):
            pairs.append(((2 * h + lane, col), (2 * h + 1 - lane, col)))
    mate = flat_permute(both, pairs, col_count)
    mine = row_id % 2 == col_id % 2
    return jnp.where(mine, both, mate)


def per_device(a_matrix, l_panels, linv):
    row_count = lax.axis_size("row")
    col_count = lax.axis_size("col")
    row_id = lax.axis_index("row")
    col_id = lax.axis_index("col")
    row_blocks = a_matrix.shape[0]
    col_blocks = a_matrix.shape[3]
    nb = a_matrix.shape[2]
    ratio = row_count // col_count
    assert ratio == 2 and row_count == ratio * col_count
    a_loc = a_matrix.reshape(row_blocks * nb, col_blocks * nb)
    l_loc = l_panels.reshape(row_blocks * nb, 2 * nb)
    width = col_blocks * nb

    top_rows = a_matrix[0].reshape(nb * col_blocks, nb)
    payload = jnp.concatenate([top_rows, l_panels[0, 0, :, :nb]], 0)
    top0, top1 = from_two_cores(payload, row_id, row_count)
    b_cols = jnp.concatenate(
        [top0[: nb * col_blocks].reshape(nb, width), top1[: nb * col_blocks].reshape(nb, width)], 0
    )
    link = top1[nb * col_blocks :]

    both = factor_sources(l_loc, row_id, col_id, row_count, col_count)
    l_cols = jnp.concatenate(
        [both[(k % ratio) * 2 * nb + (k // ratio) * nb :][:nb] for k in range(col_blocks)],
        0,
    )

    first_inverse = linv[0]
    second_inverse = linv[1]
    corner = -mm(second_inverse, mm(link, first_inverse))
    zero_block = jnp.zeros_like(first_inverse)
    k_top = jnp.concatenate(
        [
            jnp.concatenate([first_inverse, zero_block], 1),
            jnp.concatenate([corner, second_inverse], 1),
        ],
        0,
    )
    k_minus = k_top - jnp.eye(2 * nb, dtype=k_top.dtype)

    def u_rows(factor_rows, first_block):
        u = -mm(factor_rows, k_top)
        head = jnp.where(
            first_block == 0,
            k_minus[:nb],
            jnp.where(first_block == 1, k_minus[nb:], u[:nb]),
        )
        return jnp.concatenate([head, u[nb:]], 0)

    u_i = u_rows(l_loc, row_id)
    u_j = u_rows(l_cols, col_id)

    piece = a_loc[:, :nb] + mm(u_i, b_cols[:, :nb])
    half0 = jnp.where(col_id == 0, piece, jnp.zeros_like(piece))
    half1 = jnp.where(col_id == 1, piece, jnp.zeros_like(piece))
    for shift in [1] + list(reversed(range(2, col_count))):
        perm = [(h, (h + shift) % col_count) for h in range(2)]
        got = lax.ppermute(piece, "col", perm)
        half0 = jnp.where(col_id == shift, got, half0)
        half1 = jnp.where(col_id == (1 + shift) % col_count, got, half1)
    w_i = jnp.concatenate([half0, half1], 1)
    out = a_loc + mm(u_i, b_cols) + times_transposed(w_i, u_j)
    return out.reshape(a_matrix.shape)


def solution(mesh):
    in_specs = (P(None, "row", None, None, "col", None), P(None, "row", None, None), P())
    out_specs = P(None, "row", None, None, "col", None)
    return jax.shard_map(
        per_device, mesh=mesh, in_specs=in_specs, out_specs=out_specs, check_vma=False
    )
```

```python
import jax
import jax.numpy as jnp
from jax import lax
from jax.sharding import PartitionSpec as P

precise = lax.Precision.HIGHEST
AXES = ("row", "col")


def mm(left, right):
    return jnp.dot(left, right, precision=precise)


def times_transposed(left, right):
    return lax.dot_general(left, right, (((1,), (1,)), ((), ())), precision=precise)


def flat_permute(value, pairs, col_count):
    flat = [(s[0] * col_count + s[1], t[0] * col_count + t[1]) for s, t in pairs]
    return lax.ppermute(value, AXES, flat)


def cube_rounds(source_chip, bits):
    holders = [source_chip]
    rounds = []
    for bit in bits:
        step = [(h, h ^ (1 << bit)) for h in holders]
        holders = holders + [t for _, t in step]
        rounds.append(step)
    return rounds


def chip_bits(row_count):
    chips = row_count // 2
    count = chips.bit_length() - 1
    assert 1 << count == chips
    return list(range(count))


def from_two_cores(payload, row_id, row_count, col_count):
    bits = chip_bits(row_count)
    down, up = cube_rounds(0, bits[::-1]), cube_rounds(0, bits)
    held = payload
    for step in range(len(bits)):
        pairs = []
        for col in range(col_count):
            lanes = [down, up] if col % 2 == 0 else [up, down]
            for core in range(2):
                for s, t in lanes[core][step]:
                    pairs.append(((2 * s + core, col), (2 * t + core, col)))
        got = flat_permute(held, pairs, col_count)
        held = jnp.where(row_id < 2, payload, got) if step == 0 else held + got
    mate = lax.ppermute(held, "row", [(i, i ^ 1) for i in range(row_count)])
    even = row_id % 2 == 0
    return jnp.where(even, held, mate), jnp.where(even, mate, held)


def factor_sources(l_loc, row_id, col_id, row_count, col_count):
    bits = chip_bits(row_count)
    plan = []
    for col in range(col_count):
        first, second = col, col + col_count
        k1, k2 = first // 2, second // 2
        split = ((k1 ^ k2) & -(k1 ^ k2)).bit_length() - 1
        others = [b for b in bits if b != split]
        plan.append((first % 2, k1, k2, split, cube_rounds(k1, others), cube_rounds(k2, others)))
    is_source = (row_id == col_id) | (row_id == col_id + col_count)
    held = l_loc
    for step in range(len(bits) - 1):
        pairs = []
        for col, (lane, _, _, _, rounds1, rounds2) in enumerate(plan):
            for s, t in rounds1[step] + rounds2[step]:
                pairs.append(((2 * s + lane, col), (2 * t + lane, col)))
        got = flat_permute(held, pairs, col_count)
        held = jnp.where(is_source, l_loc, got) if step == 0 else held + got
    pairs = []
    for col, (lane, _, _, split, _, _) in enumerate(plan):
        for h in range(row_count // 2):
            pairs.append(((2 * h + lane, col), (2 * (h ^ (1 << split)) + lane, col)))
    other = flat_permute(held, pairs, col_count)
    split_of = jnp.array([p[3] for p in plan], jnp.int32)[col_id]
    first_side = jnp.array([p[1] for p in plan], jnp.int32)[col_id]
    in_first = ((row_id // 2) >> split_of) % 2 == (first_side >> split_of) % 2
    both = jnp.concatenate(
        [jnp.where(in_first, held, other), jnp.where(in_first, other, held)], 0
    )
    pairs = []
    for col, (lane, _, _, _, _, _) in enumerate(plan):
        for h in range(row_count // 2):
            pairs.append(((2 * h + lane, col), (2 * h + 1 - lane, col)))
    mate = flat_permute(both, pairs, col_count)
    mine = row_id % 2 == col_id % 2
    return jnp.where(mine, both, mate)


def per_device(a_matrix, l_panels, linv):
    row_count = lax.axis_size("row")
    col_count = lax.axis_size("col")
    row_id = lax.axis_index("row")
    col_id = lax.axis_index("col")
    row_blocks = a_matrix.shape[0]
    col_blocks = a_matrix.shape[3]
    nb = a_matrix.shape[2]
    ratio = row_count // col_count
    assert ratio == 2 and row_count == ratio * col_count
    a_loc = a_matrix.reshape(row_blocks * nb, col_blocks * nb)
    l_loc = l_panels.reshape(row_blocks * nb, 2 * nb)
    width = col_blocks * nb

    top_rows = a_matrix[0].reshape(nb * col_blocks, nb)
    payload = jnp.concatenate([top_rows, l_panels[0, 0, :, :nb]], 0)
    top0, top1 = from_two_cores(payload, row_id, row_count, col_count)
    b_cols = jnp.concatenate(
        [top0[: nb * col_blocks].reshape(nb, width), top1[: nb * col_blocks].reshape(nb, width)], 0
    )
    link = top1[nb * col_blocks :]

    both = factor_sources(l_loc, row_id, col_id, row_count, col_count)
    l_cols = jnp.concatenate(
        [both[(k % ratio) * 2 * nb + (k // ratio) * nb :][:nb] for k in range(col_blocks)],
        0,
    )

    first_inverse = linv[0]
    second_inverse = linv[1]
    corner = -mm(second_inverse, mm(link, first_inverse))
    zero_block = jnp.zeros_like(first_inverse)
    k_top = jnp.concatenate(
        [
            jnp.concatenate([first_inverse, zero_block], 1),
            jnp.concatenate([corner, second_inverse], 1),
        ],
        0,
    )
    k_minus = k_top - jnp.eye(2 * nb, dtype=k_top.dtype)

    def u_rows(factor_rows, first_block):
        u = -mm(factor_rows, k_top)
        head = jnp.where(
            first_block == 0,
            k_minus[:nb],
            jnp.where(first_block == 1, k_minus[nb:], u[:nb]),
        )
        return jnp.concatenate([head, u[nb:]], 0)

    u_i = u_rows(l_loc, row_id)
    u_j = u_rows(l_cols, col_id)

    piece = a_loc[:, :nb] + mm(u_i, b_cols[:, :nb])
    half0 = jnp.where(col_id == 0, piece, jnp.zeros_like(piece))
    half1 = jnp.where(col_id == 1, piece, jnp.zeros_like(piece))
    for shift in [1] + list(reversed(range(2, col_count))):
        perm = [(h, (h + shift) % col_count) for h in range(2)]
        got = lax.ppermute(piece, "col", perm)
        half0 = jnp.where(col_id == shift, got, half0)
        half1 = jnp.where(col_id == (1 + shift) % col_count, got, half1)
    w_i = jnp.concatenate([half0, half1], 1)
    out = a_loc + mm(u_i, b_cols) + times_transposed(w_i, u_j)
    return out.reshape(a_matrix.shape)


def solution(mesh):
    in_specs = (P(None, "row", None, None, "col", None), P(None, "row", None, None), P())
    out_specs = P(None, "row", None, None, "col", None)
    return jax.shard_map(
        per_device, mesh=mesh, in_specs=in_specs, out_specs=out_specs, check_vma=False
    )
```

```python
import jax
import jax.numpy as jnp
from jax import lax
from jax.sharding import PartitionSpec as P

precise = lax.Precision.HIGHEST
AXES = ("row", "col")


def mm(left, right):
    return jnp.dot(left, right, precision=precise)


def times_transposed(left, right):
    return lax.dot_general(left, right, (((1,), (1,)), ((), ())), precision=precise)


def flat_permute(value, pairs, col_count):
    flat = [(s[0] * col_count + s[1], t[0] * col_count + t[1]) for s, t in pairs]
    return lax.ppermute(value, AXES, flat)


def cube_rounds(source_chip, bits):
    holders = [source_chip]
    rounds = []
    for bit in bits:
        step = [(h, h ^ (1 << bit)) for h in holders]
        holders = holders + [t for _, t in step]
        rounds.append(step)
    return rounds


def chip_bits(row_count):
    chips = row_count // 2
    count = chips.bit_length() - 1
    assert 1 << count == chips
    return list(range(count))


def from_two_cores(payload, row_id, row_count):
    bits = chip_bits(row_count)
    lanes = [cube_rounds(0, bits[::-1]), cube_rounds(0, bits)]
    held = payload
    for step in range(len(bits)):
        perm = [
            (2 * s + core, 2 * t + core)
            for core in range(2)
            for s, t in lanes[core][step]
        ]
        got = lax.ppermute(held, "row", perm)
        held = jnp.where(row_id < 2, payload, got) if step == 0 else held + got
    mate = lax.ppermute(held, "row", [(i, i ^ 1) for i in range(row_count)])
    even = row_id % 2 == 0
    return jnp.where(even, held, mate), jnp.where(even, mate, held)


def factor_sources(l_loc, row_id, col_id, row_count, col_count):
    bits = chip_bits(row_count)
    plan = []
    for col in range(col_count):
        first, second = col, col + col_count
        k1, k2 = first // 2, second // 2
        split = ((k1 ^ k2) & -(k1 ^ k2)).bit_length() - 1
        others = [b for b in bits if b != split]
        plan.append((first % 2, k1, k2, split, cube_rounds(k1, others), cube_rounds(k2, others)))
    is_source = (row_id == col_id) | (row_id == col_id + col_count)
    held = l_loc
    for step in range(len(bits) - 1):
        pairs = []
        for col, (lane, _, _, _, rounds1, rounds2) in enumerate(plan):
            for s, t in rounds1[step] + rounds2[step]:
                pairs.append(((2 * s + lane, col), (2 * t + lane, col)))
        got = flat_permute(held, pairs, col_count)
        held = jnp.where(is_source, l_loc, got) if step == 0 else held + got
    pairs = []
    for col, (lane, _, _, split, _, _) in enumerate(plan):
        for h in range(row_count // 2):
            pairs.append(((2 * h + lane, col), (2 * (h ^ (1 << split)) + lane, col)))
    other = flat_permute(held, pairs, col_count)
    split_of = jnp.array([p[3] for p in plan], jnp.int32)[col_id]
    first_side = jnp.array([p[1] for p in plan], jnp.int32)[col_id]
    in_first = ((row_id // 2) >> split_of) % 2 == (first_side >> split_of) % 2
    both = jnp.concatenate(
        [jnp.where(in_first, held, other), jnp.where(in_first, other, held)], 0
    )
    pairs = []
    for col, (lane, _, _, _, _, _) in enumerate(plan):
        for h in range(row_count // 2):
            pairs.append(((2 * h + lane, col), (2 * h + 1 - lane, col)))
    mate = flat_permute(both, pairs, col_count)
    mine = row_id % 2 == col_id % 2
    return jnp.where(mine, both, mate)


def per_device(a_matrix, l_panels, linv):
    row_count = lax.axis_size("row")
    col_count = lax.axis_size("col")
    row_id = lax.axis_index("row")
    col_id = lax.axis_index("col")
    row_blocks = a_matrix.shape[0]
    col_blocks = a_matrix.shape[3]
    nb = a_matrix.shape[2]
    ratio = row_count // col_count
    assert ratio == 2 and row_count == ratio * col_count
    a_loc = a_matrix.reshape(row_blocks * nb, col_blocks * nb)
    l_loc = l_panels.reshape(row_blocks * nb, 2 * nb)
    width = col_blocks * nb

    top_rows = a_matrix[0].reshape(nb * col_blocks, nb)
    payload = jnp.concatenate([top_rows, l_panels[0, 0, :, :nb]], 0)
    top0, top1 = from_two_cores(payload, row_id, row_count)
    b_cols = jnp.concatenate(
        [top0[: nb * col_blocks].reshape(nb, width), top1[: nb * col_blocks].reshape(nb, width)], 0
    )
    link = top1[nb * col_blocks :]

    both = factor_sources(l_loc, row_id, col_id, row_count, col_count)
    l_cols = jnp.concatenate(
        [both[(k % ratio) * 2 * nb + (k // ratio) * nb :][:nb] for k in range(col_blocks)],
        0,
    )

    first_inverse = linv[0]
    second_inverse = linv[1]
    corner = -mm(second_inverse, mm(link, first_inverse))
    zero_block = jnp.zeros_like(first_inverse)
    k_top = jnp.concatenate(
        [
            jnp.concatenate([first_inverse, zero_block], 1),
            jnp.concatenate([corner, second_inverse], 1),
        ],
        0,
    )
    k_minus = k_top - jnp.eye(2 * nb, dtype=k_top.dtype)

    def u_rows(factor_rows, first_block):
        u = -mm(factor_rows, k_top)
        head = jnp.where(
            first_block == 0,
            k_minus[:nb],
            jnp.where(first_block == 1, k_minus[nb:], u[:nb]),
        )
        return jnp.concatenate([head, u[nb:]], 0)

    u_i = u_rows(l_loc, row_id)
    u_j = u_rows(l_cols, col_id)

    piece = a_loc[:, :nb] + mm(u_i, b_cols[:, :nb])
    half0 = jnp.where(col_id == 0, piece, jnp.zeros_like(piece))
    half1 = jnp.where(col_id == 1, piece, jnp.zeros_like(piece))
    for shift in reversed(range(1, col_count)):
        perm = [(h, (h + shift) % col_count) for h in range(2)]
        got = lax.ppermute(piece, "col", perm)
        half0 = jnp.where(col_id == shift, got, half0)
        half1 = jnp.where(col_id == (1 + shift) % col_count, got, half1)
    w_i = jnp.concatenate([half0, half1], 1)
    out = a_loc + mm(u_i, b_cols) + times_transposed(w_i, u_j)
    return out.reshape(a_matrix.shape)


def solution(mesh):
    in_specs = (P(None, "row", None, None, "col", None), P(None, "row", None, None), P())
    out_specs = P(None, "row", None, None, "col", None)
    return jax.shard_map(
        per_device, mesh=mesh, in_specs=in_specs, out_specs=out_specs, check_vma=False
    )
```

```python
import jax
import jax.numpy as jnp
from jax import lax
from jax.sharding import PartitionSpec as P

precise = lax.Precision.HIGHEST
AXES = ("row", "col")


def mm(left, right):
    return jnp.dot(left, right, precision=precise)


def times_transposed(left, right):
    return lax.dot_general(left, right, (((1,), (1,)), ((), ())), precision=precise)


def flat_permute(value, pairs, col_count):
    flat = [(s[0] * col_count + s[1], t[0] * col_count + t[1]) for s, t in pairs]
    return lax.ppermute(value, AXES, flat)


def cube_rounds(source_chip, bits):
    holders = [source_chip]
    rounds = []
    for bit in bits:
        step = [(h, h ^ (1 << bit)) for h in holders]
        holders = holders + [t for _, t in step]
        rounds.append(step)
    return rounds


def chip_bits(row_count):
    chips = row_count // 2
    count = chips.bit_length() - 1
    assert 1 << count == chips
    return list(range(count))


def from_two_cores(payload, row_id, row_count):
    bits = chip_bits(row_count)
    lanes = [cube_rounds(0, bits[::-1]), cube_rounds(0, bits)]
    held = payload
    for step in range(len(bits)):
        perm = [
            (2 * s + core, 2 * t + core)
            for core in range(2)
            for s, t in lanes[core][step]
        ]
        got = lax.ppermute(held, "row", perm)
        held = jnp.where(row_id < 2, payload, got) if step == 0 else held + got
    mate = lax.ppermute(held, "row", [(i, i ^ 1) for i in range(row_count)])
    even = row_id % 2 == 0
    return jnp.where(even, held, mate), jnp.where(even, mate, held), held


def factor_sources(l_loc, row_id, col_id, row_count, col_count):
    bits = chip_bits(row_count)
    plan = []
    for col in range(col_count):
        first, second = col, col + col_count
        k1, k2 = first // 2, second // 2
        split = ((k1 ^ k2) & -(k1 ^ k2)).bit_length() - 1
        others = [b for b in bits if b != split]
        plan.append((first % 2, k1, k2, split, cube_rounds(k1, others), cube_rounds(k2, others)))
    is_source = (row_id == col_id) | (row_id == col_id + col_count)
    held = l_loc
    for step in range(len(bits) - 1):
        pairs = []
        for col, (lane, _, _, _, rounds1, rounds2) in enumerate(plan):
            for s, t in rounds1[step] + rounds2[step]:
                pairs.append(((2 * s + lane, col), (2 * t + lane, col)))
        got = flat_permute(held, pairs, col_count)
        held = jnp.where(is_source, l_loc, got) if step == 0 else held + got
    pairs = []
    for col, (lane, _, _, split, _, _) in enumerate(plan):
        for h in range(row_count // 2):
            pairs.append(((2 * h + lane, col), (2 * (h ^ (1 << split)) + lane, col)))
    other = flat_permute(held, pairs, col_count)
    split_of = jnp.array([p[3] for p in plan], jnp.int32)[col_id]
    first_side = jnp.array([p[1] for p in plan], jnp.int32)[col_id]
    in_first = ((row_id // 2) >> split_of) % 2 == (first_side >> split_of) % 2
    both = jnp.concatenate(
        [jnp.where(in_first, held, other), jnp.where(in_first, other, held)], 0
    )
    pairs = []
    for col, (lane, _, _, _, _, _) in enumerate(plan):
        for h in range(row_count // 2):
            pairs.append(((2 * h + lane, col), (2 * h + 1 - lane, col)))
    mate = flat_permute(both, pairs, col_count)
    mine = row_id % 2 == col_id % 2
    return jnp.where(mine, both, mate)


def per_device(a_matrix, l_panels, linv):
    row_count = lax.axis_size("row")
    col_count = lax.axis_size("col")
    row_id = lax.axis_index("row")
    col_id = lax.axis_index("col")
    row_blocks = a_matrix.shape[0]
    col_blocks = a_matrix.shape[3]
    nb = a_matrix.shape[2]
    ratio = row_count // col_count
    assert ratio == 2 and row_count == ratio * col_count
    a_loc = a_matrix.reshape(row_blocks * nb, col_blocks * nb)
    l_loc = l_panels.reshape(row_blocks * nb, 2 * nb)
    width = col_blocks * nb

    top_rows = a_matrix[0].reshape(nb * col_blocks, nb)
    payload = jnp.concatenate([top_rows, l_panels[0, 0, :, :nb]], 0)
    top0, top1, held = from_two_cores(payload, row_id, row_count)
    rows_end = nb * col_blocks
    small = jnp.concatenate([held[:rows_end:col_blocks], held[rows_end:]], 0)
    small_mate = lax.ppermute(small, "row", [(i, i ^ 1) for i in range(row_count)])
    even = row_id % 2 == 0
    small0 = jnp.where(even, small, small_mate)
    small1 = jnp.where(even, small_mate, small)
    d_cols = jnp.concatenate([small0[:nb], small1[:nb]], 0)
    b_cols = jnp.concatenate(
        [top0[: nb * col_blocks].reshape(nb, width), top1[: nb * col_blocks].reshape(nb, width)], 0
    )
    link = small1[nb:]

    both = factor_sources(l_loc, row_id, col_id, row_count, col_count)
    l_cols = jnp.concatenate(
        [both[(k % ratio) * 2 * nb + (k // ratio) * nb :][:nb] for k in range(col_blocks)],
        0,
    )

    first_inverse = linv[0]
    second_inverse = linv[1]
    corner = -mm(second_inverse, mm(link, first_inverse))
    zero_block = jnp.zeros_like(first_inverse)
    k_top = jnp.concatenate(
        [
            jnp.concatenate([first_inverse, zero_block], 1),
            jnp.concatenate([corner, second_inverse], 1),
        ],
        0,
    )
    k_minus = k_top - jnp.eye(2 * nb, dtype=k_top.dtype)

    def u_rows(factor_rows, first_block):
        u = -mm(factor_rows, k_top)
        head = jnp.where(
            first_block == 0,
            k_minus[:nb],
            jnp.where(first_block == 1, k_minus[nb:], u[:nb]),
        )
        return jnp.concatenate([head, u[nb:]], 0)

    u_i = u_rows(l_loc, row_id)
    u_j = u_rows(l_cols, col_id)

    piece = a_loc[:, :nb] + mm(u_i, d_cols)
    half0 = jnp.where(col_id == 0, piece, jnp.zeros_like(piece))
    half1 = jnp.where(col_id == 1, piece, jnp.zeros_like(piece))
    for shift in [1] + list(reversed(range(2, col_count))):
        perm = [(h, (h + shift) % col_count) for h in range(2)]
        got = lax.ppermute(piece, "col", perm)
        half0 = jnp.where(col_id == shift, got, half0)
        half1 = jnp.where(col_id == (1 + shift) % col_count, got, half1)
    w_i = jnp.concatenate([half0, half1], 1)
    out = a_loc + mm(u_i, b_cols) + times_transposed(w_i, u_j)
    return out.reshape(a_matrix.shape)


def solution(mesh):
    in_specs = (P(None, "row", None, None, "col", None), P(None, "row", None, None), P())
    out_specs = P(None, "row", None, None, "col", None)
    return jax.shard_map(
        per_device, mesh=mesh, in_specs=in_specs, out_specs=out_specs, check_vma=False
    )
```

```python
import jax
import jax.numpy as jnp
from jax import lax
from jax.sharding import PartitionSpec as P

precise = lax.Precision.HIGHEST
AXES = ("row", "col")


def mm(left, right):
    return jnp.dot(left, right, precision=precise)


def times_transposed(left, right):
    return lax.dot_general(left, right, (((1,), (1,)), ((), ())), precision=precise)


def flat_permute(value, pairs, col_count):
    flat = [(s[0] * col_count + s[1], t[0] * col_count + t[1]) for s, t in pairs]
    return lax.ppermute(value, AXES, flat)


def cube_rounds(source_chip, bits):
    holders = [source_chip]
    rounds = []
    for bit in bits:
        step = [(h, h ^ (1 << bit)) for h in holders]
        holders = holders + [t for _, t in step]
        rounds.append(step)
    return rounds


def chip_bits(row_count):
    chips = row_count // 2
    count = chips.bit_length() - 1
    assert 1 << count == chips
    return list(range(count))


def from_two_cores(payload, row_id, row_count):
    bits = chip_bits(row_count)
    lanes = [cube_rounds(0, bits[::-1]), cube_rounds(0, bits)]
    held = payload
    for step in range(len(bits)):
        perm = [
            (2 * s + core, 2 * t + core)
            for core in range(2)
            for s, t in lanes[core][step]
        ]
        got = lax.ppermute(held, "row", perm)
        held = jnp.where(row_id < 2, payload, got) if step == 0 else held + got
    mate = lax.ppermute(held, "row", [(i, i ^ 1) for i in range(row_count)])
    even = row_id % 2 == 0
    return jnp.where(even, held, mate), jnp.where(even, mate, held)


def factor_sources(l_loc, row_id, col_id, row_count, col_count):
    bits = chip_bits(row_count)
    plan = []
    for col in range(col_count):
        first, second = col, col + col_count
        k1, k2 = first // 2, second // 2
        split = ((k1 ^ k2) & -(k1 ^ k2)).bit_length() - 1
        others = [b for b in bits if b != split]
        plan.append((first % 2, k1, k2, split, cube_rounds(k1, others), cube_rounds(k2, others)))
    is_source = (row_id == col_id) | (row_id == col_id + col_count)
    held = l_loc
    for step in range(len(bits) - 1):
        pairs = []
        for col, (lane, _, _, _, rounds1, rounds2) in enumerate(plan):
            for s, t in rounds1[step] + rounds2[step]:
                pairs.append(((2 * s + lane, col), (2 * t + lane, col)))
        got = flat_permute(held, pairs, col_count)
        held = jnp.where(is_source, l_loc, got) if step == 0 else held + got
    pairs = []
    for col, (lane, _, _, split, _, _) in enumerate(plan):
        for h in range(row_count // 2):
            pairs.append(((2 * h + lane, col), (2 * (h ^ (1 << split)) + lane, col)))
    other = flat_permute(held, pairs, col_count)
    split_of = jnp.array([p[3] for p in plan], jnp.int32)[col_id]
    first_side = jnp.array([p[1] for p in plan], jnp.int32)[col_id]
    in_first = ((row_id // 2) >> split_of) % 2 == (first_side >> split_of) % 2
    both = jnp.concatenate(
        [jnp.where(in_first, held, other), jnp.where(in_first, other, held)], 0
    )
    pairs = []
    for col, (lane, _, _, _, _, _) in enumerate(plan):
        for h in range(row_count // 2):
            pairs.append(((2 * h + lane, col), (2 * h + 1 - lane, col)))
    mate = flat_permute(both, pairs, col_count)
    mine = row_id % 2 == col_id % 2
    return jnp.where(mine, both, mate)


def per_device(a_matrix, l_panels, linv):
    row_count = lax.axis_size("row")
    col_count = lax.axis_size("col")
    row_id = lax.axis_index("row")
    col_id = lax.axis_index("col")
    row_blocks = a_matrix.shape[0]
    col_blocks = a_matrix.shape[3]
    nb = a_matrix.shape[2]
    ratio = row_count // col_count
    assert ratio == 2 and row_count == ratio * col_count
    a_loc = a_matrix.reshape(row_blocks * nb, col_blocks * nb)
    l_loc = l_panels.reshape(row_blocks * nb, 2 * nb)
    width = col_blocks * nb

    top_rows = a_matrix[0].reshape(nb * col_blocks, nb)
    payload = jnp.concatenate([top_rows, l_panels[0, 0, :, :nb]], 0)
    top0, top1 = from_two_cores(payload, row_id, row_count)
    b_cols = jnp.concatenate(
        [top0[: nb * col_blocks].reshape(nb, width), top1[: nb * col_blocks].reshape(nb, width)], 0
    )
    link = top1[nb * col_blocks :]

    both = factor_sources(l_loc, row_id, col_id, row_count, col_count)
    l_cols = jnp.concatenate(
        [both[(k % ratio) * 2 * nb + (k // ratio) * nb :][:nb] for k in range(col_blocks)],
        0,
    )

    first_inverse = linv[0]
    second_inverse = linv[1]
    corner = -mm(second_inverse, mm(link, first_inverse))
    zero_block = jnp.zeros_like(first_inverse)
    k_top = jnp.concatenate(
        [
            jnp.concatenate([first_inverse, zero_block], 1),
            jnp.concatenate([corner, second_inverse], 1),
        ],
        0,
    )
    k_minus = k_top - jnp.eye(2 * nb, dtype=k_top.dtype)

    def u_rows(factor_rows, first_block):
        u = -mm(factor_rows, k_top)
        head = jnp.where(
            first_block == 0,
            k_minus[:nb],
            jnp.where(first_block == 1, k_minus[nb:], u[:nb]),
        )
        return jnp.concatenate([head, u[nb:]], 0)

    u_i = u_rows(l_loc, row_id)
    u_j = u_rows(l_cols, col_id)

    piece = a_loc[:, :nb] + mm(u_i, b_cols[:, :nb])
    half0 = jnp.where(col_id == 0, piece, jnp.zeros_like(piece))
    half1 = jnp.where(col_id == 1, piece, jnp.zeros_like(piece))
    for shift in range(1, col_count):
        perm = [(h, (h + shift) % col_count) for h in range(2)]
        got = lax.ppermute(piece, "col", perm)
        half0 = jnp.where(col_id == shift, got, half0)
        half1 = jnp.where(col_id == (1 + shift) % col_count, got, half1)
    w_i = jnp.concatenate([half0, half1], 1)
    out = a_loc + mm(u_i, b_cols) + times_transposed(w_i, u_j)
    return out.reshape(a_matrix.shape)


def solution(mesh):
    in_specs = (P(None, "row", None, None, "col", None), P(None, "row", None, None), P())
    out_specs = P(None, "row", None, None, "col", None)
    return jax.shard_map(
        per_device, mesh=mesh, in_specs=in_specs, out_specs=out_specs, check_vma=False
    )
```

```python
import jax
import jax.numpy as jnp
from jax import lax
from jax.sharding import PartitionSpec as P

precise = lax.Precision.HIGHEST
AXES = ("row", "col")


def mm(left, right):
    return jnp.dot(left, right, precision=precise)


def times_transposed(left, right):
    return lax.dot_general(left, right, (((1,), (1,)), ((), ())), precision=precise)


def flat_permute(value, pairs, col_count):
    flat = [(s[0] * col_count + s[1], t[0] * col_count + t[1]) for s, t in pairs]
    return lax.ppermute(value, AXES, flat)


def cube_rounds(source_chip, bits):
    holders = [source_chip]
    rounds = []
    for bit in bits:
        step = [(h, h ^ (1 << bit)) for h in holders]
        holders = holders + [t for _, t in step]
        rounds.append(step)
    return rounds


def chip_bits(row_count):
    chips = row_count // 2
    count = chips.bit_length() - 1
    assert 1 << count == chips
    return list(range(count))


def from_two_cores(payload, row_id, row_count):
    bits = chip_bits(row_count)
    lanes = [cube_rounds(0, bits[::-1]), cube_rounds(0, bits)]
    held = payload
    for step in range(len(bits)):
        perm = [
            (2 * s + core, 2 * t + core)
            for core in range(2)
            for s, t in lanes[core][step]
        ]
        got = lax.ppermute(held, "row", perm)
        held = jnp.where(row_id < 2, payload, got) if step == 0 else held + got
    mate = lax.ppermute(held, "row", [(i, i ^ 1) for i in range(row_count)])
    even = row_id % 2 == 0
    return jnp.where(even, held, mate), jnp.where(even, mate, held)


def factor_sources(l_loc, row_id, col_id, row_count, col_count):
    bits = chip_bits(row_count)
    plan = []
    for col in range(col_count):
        first, second = col, col + col_count
        k1, k2 = first // 2, second // 2
        split = ((k1 ^ k2) & -(k1 ^ k2)).bit_length() - 1
        others = [b for b in bits if b != split]
        plan.append((first % 2, k1, k2, split, cube_rounds(k1, others), cube_rounds(k2, others)))
    is_source = (row_id == col_id) | (row_id == col_id + col_count)
    held = l_loc
    for step in range(len(bits) - 1):
        pairs = []
        for col, (lane, _, _, _, rounds1, rounds2) in enumerate(plan):
            for s, t in rounds1[step] + rounds2[step]:
                pairs.append(((2 * s + lane, col), (2 * t + lane, col)))
        got = flat_permute(held, pairs, col_count)
        held = jnp.where(is_source, l_loc, got) if step == 0 else held + got
    pairs = []
    for col, (lane, _, _, split, _, _) in enumerate(plan):
        for h in range(row_count // 2):
            pairs.append(((2 * h + lane, col), (2 * (h ^ (1 << split)) + lane, col)))
    other = flat_permute(held, pairs, col_count)
    split_of = jnp.array([p[3] for p in plan], jnp.int32)[col_id]
    first_side = jnp.array([p[1] for p in plan], jnp.int32)[col_id]
    in_first = ((row_id // 2) >> split_of) % 2 == (first_side >> split_of) % 2
    both = jnp.concatenate(
        [jnp.where(in_first, held, other), jnp.where(in_first, other, held)], 0
    )
    pairs = []
    for col, (lane, _, _, _, _, _) in enumerate(plan):
        for h in range(row_count // 2):
            pairs.append(((2 * h + lane, col), (2 * h + 1 - lane, col)))
    mate = flat_permute(both, pairs, col_count)
    mine = row_id % 2 == col_id % 2
    return jnp.where(mine, both, mate)


def per_device(a_matrix, l_panels, linv):
    row_count = lax.axis_size("row")
    col_count = lax.axis_size("col")
    row_id = lax.axis_index("row")
    col_id = lax.axis_index("col")
    row_blocks = a_matrix.shape[0]
    col_blocks = a_matrix.shape[3]
    nb = a_matrix.shape[2]
    ratio = row_count // col_count
    assert ratio == 2 and row_count == ratio * col_count
    a_loc = a_matrix.reshape(row_blocks * nb, col_blocks * nb)
    l_loc = l_panels.reshape(row_blocks * nb, 2 * nb)
    width = col_blocks * nb

    top_rows = a_matrix[0].reshape(nb * col_blocks, nb)
    first_inverse = linv[0]
    second_inverse = linv[1]
    corner_here = -mm(second_inverse, mm(l_panels[0, 0, :, :nb], first_inverse))
    payload = jnp.concatenate([top_rows, corner_here], 0)
    top0, top1 = from_two_cores(payload, row_id, row_count)
    b_cols = jnp.concatenate(
        [top0[: nb * col_blocks].reshape(nb, width), top1[: nb * col_blocks].reshape(nb, width)], 0
    )
    corner = top1[nb * col_blocks :]

    both = factor_sources(l_loc, row_id, col_id, row_count, col_count)
    l_cols = jnp.concatenate(
        [both[(k % ratio) * 2 * nb + (k // ratio) * nb :][:nb] for k in range(col_blocks)],
        0,
    )

    zero_block = jnp.zeros_like(first_inverse)
    k_top = jnp.concatenate(
        [
            jnp.concatenate([first_inverse, zero_block], 1),
            jnp.concatenate([corner, second_inverse], 1),
        ],
        0,
    )
    k_minus = k_top - jnp.eye(2 * nb, dtype=k_top.dtype)

    def u_rows(factor_rows, first_block):
        u = -mm(factor_rows, k_top)
        head = jnp.where(
            first_block == 0,
            k_minus[:nb],
            jnp.where(first_block == 1, k_minus[nb:], u[:nb]),
        )
        return jnp.concatenate([head, u[nb:]], 0)

    u_i = u_rows(l_loc, row_id)
    u_j = u_rows(l_cols, col_id)

    piece = a_loc[:, :nb] + mm(u_i, b_cols[:, :nb])
    half0 = jnp.where(col_id == 0, piece, jnp.zeros_like(piece))
    half1 = jnp.where(col_id == 1, piece, jnp.zeros_like(piece))
    for shift in range(1, col_count):
        perm = [(h, (h + shift) % col_count) for h in range(2)]
        got = lax.ppermute(piece, "col", perm)
        half0 = jnp.where(col_id == shift, got, half0)
        half1 = jnp.where(col_id == (1 + shift) % col_count, got, half1)
    w_i = jnp.concatenate([half0, half1], 1)
    out = a_loc + mm(u_i, b_cols) + times_transposed(w_i, u_j)
    return out.reshape(a_matrix.shape)


def solution(mesh):
    in_specs = (P(None, "row", None, None, "col", None), P(None, "row", None, None), P())
    out_specs = P(None, "row", None, None, "col", None)
    return jax.shard_map(
        per_device, mesh=mesh, in_specs=in_specs, out_specs=out_specs, check_vma=False
    )
```

```python
import jax
import jax.numpy as jnp
from jax import lax
from jax.sharding import PartitionSpec as P

precise = lax.Precision.HIGHEST
AXES = ("row", "col")


def mm(left, right):
    return jnp.dot(left, right, precision=precise)


def times_transposed(left, right):
    return lax.dot_general(left, right, (((1,), (1,)), ((), ())), precision=precise)


def flat_permute(value, pairs, col_count):
    flat = [(s[0] * col_count + s[1], t[0] * col_count + t[1]) for s, t in pairs]
    return lax.ppermute(value, AXES, flat)


def cube_rounds(source_chip, bits):
    holders = [source_chip]
    rounds = []
    for bit in bits:
        step = [(h, h ^ (1 << bit)) for h in holders]
        holders = holders + [t for _, t in step]
        rounds.append(step)
    return rounds


def chip_bits(row_count):
    chips = row_count // 2
    count = chips.bit_length() - 1
    assert 1 << count == chips
    return list(range(count))


def from_two_cores(payload, row_id, row_count, col_count):
    bits = chip_bits(row_count)
    down, up = cube_rounds(0, bits[::-1]), cube_rounds(0, bits)
    held = payload
    for step in range(len(bits)):
        pairs = []
        for col in range(col_count):
            lanes = [down, up] if col % 2 == 0 else [up, down]
            for core in range(2):
                for s, t in lanes[core][step]:
                    pairs.append(((2 * s + core, col), (2 * t + core, col)))
        got = flat_permute(held, pairs, col_count)
        held = jnp.where(row_id < 2, payload, got) if step == 0 else held + got
    mate = lax.ppermute(held, "row", [(i, i ^ 1) for i in range(row_count)])
    even = row_id % 2 == 0
    return jnp.where(even, held, mate), jnp.where(even, mate, held)


def factor_sources(l_loc, row_id, col_id, row_count, col_count):
    bits = chip_bits(row_count)
    plan = []
    for col in range(col_count):
        first, second = col, col + col_count
        k1, k2 = first // 2, second // 2
        split = ((k1 ^ k2) & -(k1 ^ k2)).bit_length() - 1
        others = [b for b in bits if b != split]
        plan.append((first % 2, k1, k2, split, cube_rounds(k1, others), cube_rounds(k2, others)))
    is_source = (row_id == col_id) | (row_id == col_id + col_count)
    held = l_loc
    for step in range(len(bits) - 1):
        pairs = []
        for col, (lane, _, _, _, rounds1, rounds2) in enumerate(plan):
            for s, t in rounds1[step] + rounds2[step]:
                pairs.append(((2 * s + lane, col), (2 * t + lane, col)))
        got = flat_permute(held, pairs, col_count)
        held = jnp.where(is_source, l_loc, got) if step == 0 else held + got
    pairs = []
    for col, (lane, _, _, split, _, _) in enumerate(plan):
        for h in range(row_count // 2):
            pairs.append(((2 * h + lane, col), (2 * (h ^ (1 << split)) + lane, col)))
    other = flat_permute(held, pairs, col_count)
    split_of = jnp.array([p[3] for p in plan], jnp.int32)[col_id]
    first_side = jnp.array([p[1] for p in plan], jnp.int32)[col_id]
    in_first = ((row_id // 2) >> split_of) % 2 == (first_side >> split_of) % 2
    both = jnp.concatenate(
        [jnp.where(in_first, held, other), jnp.where(in_first, other, held)], 0
    )
    pairs = []
    for col, (lane, _, _, _, _, _) in enumerate(plan):
        for h in range(row_count // 2):
            pairs.append(((2 * h + lane, col), (2 * h + 1 - lane, col)))
    mate = flat_permute(both, pairs, col_count)
    mine = row_id % 2 == col_id % 2
    return jnp.where(mine, both, mate)


def per_device(a_matrix, l_panels, linv):
    row_count = lax.axis_size("row")
    col_count = lax.axis_size("col")
    row_id = lax.axis_index("row")
    col_id = lax.axis_index("col")
    row_blocks = a_matrix.shape[0]
    col_blocks = a_matrix.shape[3]
    nb = a_matrix.shape[2]
    ratio = row_count // col_count
    assert ratio == 2 and row_count == ratio * col_count
    a_loc = a_matrix.reshape(row_blocks * nb, col_blocks * nb)
    l_loc = l_panels.reshape(row_blocks * nb, 2 * nb)
    width = col_blocks * nb

    top_rows = a_matrix[0].reshape(nb * col_blocks, nb)
    payload = jnp.concatenate([top_rows, l_panels[0, 0, :, :nb]], 0)
    top0, top1 = from_two_cores(payload, row_id, row_count, col_count)
    b_cols = jnp.concatenate(
        [top0[: nb * col_blocks].reshape(nb, width), top1[: nb * col_blocks].reshape(nb, width)], 0
    )
    link = top1[nb * col_blocks :]

    both = factor_sources(l_loc, row_id, col_id, row_count, col_count)
    l_cols = jnp.concatenate(
        [both[(k % ratio) * 2 * nb + (k // ratio) * nb :][:nb] for k in range(col_blocks)],
        0,
    )

    first_inverse = linv[0]
    second_inverse = linv[1]
    corner = -mm(second_inverse, mm(link, first_inverse))
    zero_block = jnp.zeros_like(first_inverse)
    k_top = jnp.concatenate(
        [
            jnp.concatenate([first_inverse, zero_block], 1),
            jnp.concatenate([corner, second_inverse], 1),
        ],
        0,
    )
    k_minus = k_top - jnp.eye(2 * nb, dtype=k_top.dtype)

    def u_rows(factor_rows, first_block):
        u = -mm(factor_rows, k_top)
        head = jnp.where(
            first_block == 0,
            k_minus[:nb],
            jnp.where(first_block == 1, k_minus[nb:], u[:nb]),
        )
        return jnp.concatenate([head, u[nb:]], 0)

    u_i = u_rows(l_loc, row_id)
    u_j = u_rows(l_cols, col_id)

    piece = a_loc[:, :nb] + mm(u_i, b_cols[:, :nb])
    half0 = jnp.where(col_id == 0, piece, jnp.zeros_like(piece))
    half1 = jnp.where(col_id == 1, piece, jnp.zeros_like(piece))
    for shift in range(1, col_count):
        perm = [(h, (h + shift) % col_count) for h in range(2)]
        got = lax.ppermute(piece, "col", perm)
        half0 = jnp.where(col_id == shift, got, half0)
        half1 = jnp.where(col_id == (1 + shift) % col_count, got, half1)
    w_i = jnp.concatenate([half0, half1], 1)
    out = a_loc + mm(u_i, b_cols) + times_transposed(w_i, u_j)
    return out.reshape(a_matrix.shape)


def solution(mesh):
    in_specs = (P(None, "row", None, None, "col", None), P(None, "row", None, None), P())
    out_specs = P(None, "row", None, None, "col", None)
    return jax.shard_map(
        per_device, mesh=mesh, in_specs=in_specs, out_specs=out_specs, check_vma=False
    )
```
